32 devices in a mesh: lat: 8 (over y, x, core), lon: 4 (over z).
Axes of the slice: x: 2, y: 2, z: 4, core: 2. Of those that a mesh axis runs over, the one named last changes fastest.
Arguments:
- spec_coef: bfloat16 [1280, 2, 64, 1280], P(('lat', 'lon')), may hold values from -0.119628906 to 0.119628906
- legendre: bfloat16 [1280, 128, 1280], P(('lat', 'lon')), may hold values from -0.15625 to 0.15625
- wave_ids: int32 [1280], replicated, may hold values from 0 to 1279, each once
- dep_drow: int32 [128, 5120], P('lat', 'lon'), may hold values from -1 to 1
- dep_dlon: int32 [128, 5120], P('lat', 'lon'), may hold values from -1 to 1
- dep_frac: float32 [2, 128, 5120], P(None, 'lat', 'lon'), may hold values from 0 to 1
Outputs:
- grid: bfloat16 [64, 128, 5120], P(None, 'lat', 'lon')
- departed: bfloat16 [64, 128, 5120], P(None, 'lat', 'lon')
The draws below stay inside these ranges and needn't reach their ends.
Inputs may be any that keep to these rules, and one draw needn't show every extreme that they name: `wave_ids`: each zonal wavenumber 0 to 1279 stands in exactly one storage row.
All inputs are finite; a program needn't handle non-finite values.
Results may differ from the reference program's by a relative error of at most 0.0059.
Values may be sent and summed in bfloat16 or wider, within the bound.
No kernel may reach another device: no remote copies, remote signals or barrier semaphores. Data moves between devices by JAX's collectives and lax.ppermute only.
A program may use at most 128 MiB of HBM per device.

```python
import math
import jax
import jax.numpy as jnp
from jax import lax

M = 1280
NT = 1280
REACH = 1
K = 64
LATS = 128
NLON = 5120


def touch_ends(result, rng, least, largest):
    longest = result.shape.index(max(result.shape))
    spots = []
    for shift in (0, 1):
        where = [jax.random.randint(jax.random.fold_in(rng, axis), (), 0, length) for axis, length in enumerate(result.shape)]
        where[longest] = (where[longest] + shift) % result.shape[longest]
        spots.append(tuple(where))
    return result.at[spots[0]].set(least).at[spots[1]].set(largest)


def levels(own_key, shape, shards, smallest, top_value):
    level = 1.0
    for axis_at, parts in shards:
        draws = jax.random.uniform(jax.random.fold_in(jax.random.fold_in(own_key, 6), axis_at), (parts,), jnp.float32, smallest / len(shards), top_value / len(shards))
        level = level * jnp.repeat(jnp.exp(draws), shape[axis_at] // parts).reshape((-1,) + (1,) * (len(shape) - 1 - axis_at))
    return level


def normal_values(stream_key, shape, deviation, reach, shards=(), held_as=jnp.bfloat16):
    drawn = jax.random.normal(stream_key, shape, jnp.float32) * deviation
    if len(shards) > 0:
        drawn = levels(stream_key, shape, shards, -0.22, 0.18) * drawn
    return jnp.clip(drawn, min=-reach, max=reach).astype(held_as)


def setup_inputs(seed: int = 0) -> dict:
    key_of = jax.random.split(jax.random.key(seed), 7)
    return {
        "spec_coef": normal_values(key_of[0], (M, 2, K, NT), 0.02, 0.119628906, ((0, 32),)),
        "legendre": normal_values(key_of[1], (M, LATS, NT), NT ** -0.5, 0.15625, ((0, 32),)),
        "wave_ids": jax.random.permutation(key_of[2], M).astype(jnp.int32),
        "dep_drow": touch_ends(jax.random.randint(key_of[3], (LATS, NLON), 0 - REACH, REACH + 1), jax.random.fold_in(key_of[3], 1), 0 - REACH, REACH).astype(jnp.int32),
        "dep_dlon": touch_ends(jax.random.randint(key_of[4], (LATS, NLON), 0 - REACH, REACH + 1), jax.random.fold_in(key_of[4], 1), 0 - REACH, REACH).astype(jnp.int32),
        "dep_frac": jnp.clip(1.0 * jax.random.uniform(key_of[5], (2, LATS, NLON), jnp.float32) ** levels(key_of[5], (2, LATS, NLON), ((1, 8), (2, 4)), -0.2, 0.2), 0.0, 1.0),
    }


def wave_table(wave_order, lon_start, lon_count, cycle_size):
    longitude = lon_start + jnp.arange(lon_count, dtype=jnp.int32)
    phase_index = (wave_order[:, None] * longitude[None, :]) % cycle_size
    theta = phase_index.astype(jnp.float32) * (2.0 * math.pi / cycle_size)
    factor = jnp.where(wave_order == 0, 1.0, 2.0).astype(jnp.float32)[:, None]
    return jnp.stack([factor * jnp.cos(theta), -factor * jnp.sin(theta)]).astype(jnp.bfloat16)


def legendre_row(inputs):
    coeffs, matrix, wavenumber = inputs
    keep = jnp.arange(NT, dtype=jnp.int32) >= wavenumber
    kept = jnp.where(keep, coeffs, jnp.zeros((), coeffs.dtype))
    product = jnp.einsum('rkn,ln->lrk', kept.astype(jnp.float32), matrix.astype(jnp.float32), precision=lax.Precision.HIGHEST)
    return product.astype(jnp.bfloat16)


def reference(spec_coef, legendre, wave_ids, dep_drow, dep_dlon, dep_frac):
    fourier = lax.map(legendre_row, (spec_coef, legendre, wave_ids))
    table = wave_table(wave_ids, 0, NLON, NLON)
    grid = jnp.einsum('mlrk,rmx->klx', fourier.astype(jnp.float32), table.astype(jnp.float32), precision=lax.Precision.HIGHEST).astype(jnp.bfloat16)
    margin = REACH + 1
    padded = jnp.pad(grid, ((0, 0), (margin, margin), (0, 0))).reshape(K, -1)
    row_index = jnp.arange(LATS, dtype=jnp.int32)[:, None]
    col_index = jnp.arange(NLON, dtype=jnp.int32)[None, :]
    frac_row = dep_frac[0]
    frac_col = dep_frac[1]
    total = jnp.zeros((K, LATS, NLON), jnp.float32)
    for upper in (0, 1):
        for right in (0, 1):
            source_row = row_index + dep_drow + upper + margin
            source_col = (col_index + dep_dlon + right) % NLON
            flat_index = (source_row * NLON + source_col).reshape(-1).astype(jnp.int32)
            values = jnp.take(padded, flat_index, axis=1).reshape(K, LATS, NLON)
            weight_row = frac_row if upper else 1.0 - frac_row
            weight_col = frac_col if right else 1.0 - frac_col
            total = total + (weight_row * weight_col)[None] * values.astype(jnp.float32)
    return grid, total.astype(jnp.bfloat16)
```

```python
import math

import jax
import jax.numpy as jnp
from jax import lax
from jax.experimental import pallas as pl
from jax.experimental.pallas import tpu as pltpu
from jax.sharding import PartitionSpec as P

REACH = 1


def padded_2(cells, sides, width, closed):
    for axis, dim in sides:
        count = lax.axis_size(axis)
        ends = count if closed else count - 1
        head = lax.slice_in_dim(cells, 0, width, axis=dim)
        tail = lax.slice_in_dim(cells, cells.shape[dim] - width, cells.shape[dim], axis=dim)
        cells = jnp.concatenate(
            [
                lax.ppermute(tail, axis, [(i, (i + 1) % count) for i in range(ends)]),
                cells,
                lax.ppermute(head, axis, [((i + 1) % count, i) for i in range(ends)]),
            ],
            axis=dim,
        )
    return cells


def wave_table(wave_order, lon_start, lon_count, cycle_size):
    longitude = lon_start + jnp.arange(lon_count, dtype=jnp.int32)
    phase_index = wave_order[:, None] * longitude[None, :] % cycle_size
    theta = phase_index.astype(jnp.float32) * (2.0 * math.pi / cycle_size)
    factor = jnp.where(wave_order == 0, 1.0, 2.0).astype(jnp.float32)[:, None]
    return jnp.stack([factor * jnp.cos(theta), -factor * jnp.sin(theta)]).astype(jnp.bfloat16)


def shift_weight(offsets, frac, shift):
    zeros = jnp.zeros_like(frac)
    lower = jnp.where(offsets == shift, 1.0 - frac, zeros)
    higher = jnp.where(offsets == shift - 1, frac, zeros)
    return lower + higher


def _block_size(count):
    for size in (8, 5, 4, 2, 1):
        if count % size == 0:
            return size
    return 1


def legendre_kernel(ids_ref, coef_ref, leg_ref, out_ref):
    step = pl.program_id(0)
    block = coef_ref.shape[0]
    bands = out_ref.shape[0]
    rows = out_ref.shape[2]
    degree_count = coef_ref.shape[2]
    degree = lax.broadcasted_iota(jnp.int32, (1, degree_count), 1)
    for w in range(block):
        wave = ids_ref[step * block + w]
        coef = coef_ref[w]
        kept = jnp.where(degree >= wave, coef, jnp.zeros((), coef.dtype))
        prod = lax.dot_general(
            leg_ref[w], kept, (((1,), (1,)), ((), ())), preferred_element_type=jnp.float32
        )
        out_ref[:, w, :, :] = prod.astype(out_ref.dtype).reshape(bands, rows, prod.shape[1])


def legendre_transform(local_ids, coef, leg, bands):
    local_waves, width, degree_count = coef.shape
    lats = leg.shape[1]
    rows = lats // bands
    block = _block_size(local_waves)
    return pl.pallas_call(
        legendre_kernel,
        out_shape=jax.ShapeDtypeStruct((bands, local_waves, rows, width), jnp.bfloat16),
        grid_spec=pltpu.PrefetchScalarGridSpec(
            num_scalar_prefetch=1,
            grid=(local_waves // block,),
            in_specs=[
                pl.BlockSpec((block, width, degree_count), lambda i, ids: (i, 0, 0)),
                pl.BlockSpec((block, lats, degree_count), lambda i, ids: (i, 0, 0)),
            ],
            out_specs=pl.BlockSpec((bands, block, rows, width), lambda i, ids: (0, i, 0, 0)),
        ),
    )(local_ids, coef, leg)


def per_device(spec_coef, legendre, wave_ids, dep_drow, dep_dlon, dep_frac):
    lat_count = lax.axis_size("lat")
    lon_parts = lax.axis_size("lon")
    local_waves = spec_coef.shape[0]
    level_fields = spec_coef.shape[2]
    degree_count = spec_coef.shape[3]
    all_waves = wave_ids.shape[0]
    row_count = dep_drow.shape[0]
    sector_width = dep_drow.shape[1]
    cycle_size = sector_width * lon_parts
    device = lax.axis_index("lat") * lon_parts + lax.axis_index("lon")
    local_ids = lax.dynamic_slice_in_dim(wave_ids, device * local_waves, local_waves)
    coef = spec_coef.reshape(local_waves, 2 * level_fields, degree_count)
    fourier = legendre_transform(local_ids, coef, legendre, lat_count)
    moved = lax.all_to_all(fourier, "lat", split_axis=0, concat_axis=0, tiled=True)
    gathered = lax.all_gather(moved, "lon", axis=0, tiled=True)
    gathered = gathered.reshape(all_waves, row_count, 2, level_fields)
    wave_order = (
        wave_ids.reshape(lat_count, lon_parts, local_waves).transpose(1, 0, 2).reshape(all_waves)
    )
    table = wave_table(wave_order, lax.axis_index("lon") * sector_width, sector_width, cycle_size)
    grid = jnp.einsum(
        "mprq,rmx->qpx", gathered, table, preferred_element_type=jnp.float32
    ).astype(jnp.bfloat16)
    margin = REACH + 1
    tall = padded_2(grid, (("lat", 1),), margin, False)
    padded = padded_2(tall, (("lon", 2),), margin, True)
    frac_row = dep_frac[0]
    frac_col = dep_frac[1]
    col_weights = [shift_weight(dep_dlon, frac_col, shift) for shift in range(-REACH, REACH + 2)]
    total = jnp.zeros((level_fields, row_count, sector_width), jnp.float32)
    for row_shift in range(-REACH, REACH + 2):
        band = padded[:, margin + row_shift : margin + row_shift + row_count, :]
        along = jnp.zeros((level_fields, row_count, sector_width), jnp.float32)
        for place, col_shift in enumerate(range(-REACH, REACH + 2)):
            window = band[:, :, margin + col_shift : margin + col_shift + sector_width].astype(
                jnp.float32
            )
            along = along + col_weights[place][None] * window
        total = total + shift_weight(dep_drow, frac_row, row_shift)[None] * along
    return (grid, total.astype(jnp.bfloat16))


def solution(mesh):
    in_specs = (
        P(("lat", "lon"), None, None, None),
        P(("lat", "lon"), None, None),
        P(),
        P("lat", "lon"),
        P("lat", "lon"),
        P(None, "lat", "lon"),
    )
    out_specs = (P(None, "lat", "lon"), P(None, "lat", "lon"))
    return jax.shard_map(
        per_device, mesh=mesh, in_specs=in_specs, out_specs=out_specs, check_vma=False
    )
```

```python
import math

import jax
import jax.numpy as jnp
from jax import lax
from jax.experimental import pallas as pl
from jax.experimental.pallas import tpu as pltpu
from jax.sharding import PartitionSpec as P

REACH = 1


def padded_2(cells, sides, width, closed):
    for axis, dim in sides:
        count = lax.axis_size(axis)
        ends = count if closed else count - 1
        head = lax.slice_in_dim(cells, 0, width, axis=dim)
        tail = lax.slice_in_dim(cells, cells.shape[dim] - width, cells.shape[dim], axis=dim)
        cells = jnp.concatenate(
            [
                lax.ppermute(tail, axis, [(i, (i + 1) % count) for i in range(ends)]),
                cells,
                lax.ppermute(head, axis, [((i + 1) % count, i) for i in range(ends)]),
            ],
            axis=dim,
        )
    return cells


def wave_table(wave_order, lon_start, lon_count, cycle_size):
    inner = 128 if lon_count % 128 == 0 else lon_count
    outer = lon_count // inner
    coarse = lon_start + inner * jnp.arange(outer, dtype=jnp.int32)
    fine = jnp.arange(inner, dtype=jnp.int32)
    scale = 2.0 * math.pi / cycle_size
    theta_a = (wave_order[:, None] * coarse[None, :] % cycle_size).astype(jnp.float32) * scale
    theta_b = (wave_order[:, None] * fine[None, :] % cycle_size).astype(jnp.float32) * scale
    cos_a = jnp.cos(theta_a)[:, :, None]
    sin_a = jnp.sin(theta_a)[:, :, None]
    cos_b = jnp.cos(theta_b)[:, None, :]
    sin_b = jnp.sin(theta_b)[:, None, :]
    factor = jnp.where(wave_order == 0, 1.0, 2.0).astype(jnp.float32)[:, None, None]
    real = factor * (cos_a * cos_b - sin_a * sin_b)
    imag = -factor * (sin_a * cos_b + cos_a * sin_b)
    count = wave_order.shape[0]
    return jnp.stack([real.reshape(count, lon_count), imag.reshape(count, lon_count)]).astype(
        jnp.bfloat16
    )


def shift_weight(offsets, frac, shift):
    zeros = jnp.zeros_like(frac)
    lower = jnp.where(offsets == shift, 1.0 - frac, zeros)
    higher = jnp.where(offsets == shift - 1, frac, zeros)
    return lower + higher


def _block_size(count):
    for size in (8, 5, 4, 2, 1):
        if count % size == 0:
            return size
    return 1


def legendre_kernel(ids_ref, coef_ref, leg_ref, out_ref):
    step = pl.program_id(0)
    block = coef_ref.shape[0]
    bands = out_ref.shape[1]
    rows = out_ref.shape[3]
    degree_count = coef_ref.shape[2]
    degree = lax.broadcasted_iota(jnp.int32, (1, degree_count), 1)
    for w in range(block):
        wave = ids_ref[step * block + w]
        coef = coef_ref[w]
        kept = jnp.where(degree >= wave, coef, jnp.zeros((), coef.dtype))
        prod = lax.dot_general(
            leg_ref[w], kept, (((1,), (1,)), ((), ())), preferred_element_type=jnp.float32
        )
        out_ref[0, :, w, :, :] = prod.astype(out_ref.dtype).reshape(bands, rows, prod.shape[1])


def legendre_transform(local_ids, coef, leg, bands, chunks):
    local_waves, width, degree_count = coef.shape
    lats = leg.shape[1]
    rows = lats // bands
    chunk_waves = local_waves // chunks
    block = _block_size(chunk_waves)
    per_chunk = chunk_waves // block
    return pl.pallas_call(
        legendre_kernel,
        out_shape=jax.ShapeDtypeStruct((chunks, bands, chunk_waves, rows, width), jnp.bfloat16),
        grid_spec=pltpu.PrefetchScalarGridSpec(
            num_scalar_prefetch=1,
            grid=(local_waves // block,),
            in_specs=[
                pl.BlockSpec((block, width, degree_count), lambda i, ids: (i, 0, 0)),
                pl.BlockSpec((block, lats, degree_count), lambda i, ids: (i, 0, 0)),
            ],
            out_specs=pl.BlockSpec(
                (1, bands, block, rows, width),
                lambda i, ids: (i // per_chunk, 0, i % per_chunk, 0, 0),
            ),
        ),
    )(local_ids, coef, leg)


def per_device(spec_coef, legendre, wave_ids, dep_drow, dep_dlon, dep_frac):
    lat_count = lax.axis_size("lat")
    lon_parts = lax.axis_size("lon")
    local_waves = spec_coef.shape[0]
    level_fields = spec_coef.shape[2]
    degree_count = spec_coef.shape[3]
    all_waves = wave_ids.shape[0]
    row_count = dep_drow.shape[0]
    sector_width = dep_drow.shape[1]
    cycle_size = sector_width * lon_parts
    device = lax.axis_index("lat") * lon_parts + lax.axis_index("lon")
    local_ids = lax.dynamic_slice_in_dim(wave_ids, device * local_waves, local_waves)
    coef = spec_coef.reshape(local_waves, 2 * level_fields, degree_count)
    chunks = 2 if local_waves % 2 == 0 else 1
    chunk_waves = local_waves // chunks
    fourier = legendre_transform(local_ids, coef, legendre, lat_count, chunks)
    lon_start = lax.axis_index("lon") * sector_width
    by_chunk = wave_ids.reshape(lat_count, lon_parts, chunks, chunk_waves)
    total = None
    for c in range(chunks):
        moved = lax.all_to_all(fourier[c], "lat", split_axis=0, concat_axis=0, tiled=True)
        gathered = lax.all_gather(moved, "lon", axis=0, tiled=True)
        gathered = gathered.reshape(lon_parts * lat_count * chunk_waves, row_count, 2, level_fields)
        wave_order = by_chunk[:, :, c, :].transpose(1, 0, 2).reshape(-1)
        table = wave_table(wave_order, lon_start, sector_width, cycle_size)
        part = jnp.einsum("mprq,rmx->qpx", gathered, table, preferred_element_type=jnp.float32)
        total = part if total is None else total + part
    grid = total.astype(jnp.bfloat16)
    margin = REACH + 1
    tall = padded_2(grid, (("lat", 1),), margin, False)
    padded = padded_2(tall, (("lon", 2),), margin, True)
    frac_row = dep_frac[0]
    frac_col = dep_frac[1]
    col_weights = [shift_weight(dep_dlon, frac_col, shift) for shift in range(-REACH, REACH + 2)]
    total = jnp.zeros((level_fields, row_count, sector_width), jnp.float32)
    for row_shift in range(-REACH, REACH + 2):
        band = padded[:, margin + row_shift : margin + row_shift + row_count, :]
        along = jnp.zeros((level_fields, row_count, sector_width), jnp.float32)
        for place, col_shift in enumerate(range(-REACH, REACH + 2)):
            window = band[:, :, margin + col_shift : margin + col_shift + sector_width].astype(
                jnp.float32
            )
            along = along + col_weights[place][None] * window
        total = total + shift_weight(dep_drow, frac_row, row_shift)[None] * along
    return (grid, total.astype(jnp.bfloat16))


def solution(mesh):
    in_specs = (
        P(("lat", "lon"), None, None, None),
        P(("lat", "lon"), None, None),
        P(),
        P("lat", "lon"),
        P("lat", "lon"),
        P(None, "lat", "lon"),
    )
    out_specs = (P(None, "lat", "lon"), P(None, "lat", "lon"))
    return jax.shard_map(
        per_device, mesh=mesh, in_specs=in_specs, out_specs=out_specs, check_vma=False
    )
```

```python
import math

import jax
import jax.numpy as jnp
from jax import lax
from jax.experimental import pallas as pl
from jax.experimental.pallas import tpu as pltpu
from jax.sharding import PartitionSpec as P

REACH = 1


def padded_2(cells, sides, width, closed):
    for axis, dim in sides:
        count = lax.axis_size(axis)
        ends = count if closed else count - 1
        head = lax.slice_in_dim(cells, 0, width, axis=dim)
        tail = lax.slice_in_dim(cells, cells.shape[dim] - width, cells.shape[dim], axis=dim)
        cells = jnp.concatenate(
            [
                lax.ppermute(tail, axis, [(i, (i + 1) % count) for i in range(ends)]),
                cells,
                lax.ppermute(head, axis, [((i + 1) % count, i) for i in range(ends)]),
            ],
            axis=dim,
        )
    return cells


def wave_table(wave_order, lon_start, lon_count, cycle_size):
    inner = 128 if lon_count % 128 == 0 else lon_count
    outer = lon_count // inner
    coarse = lon_start + inner * jnp.arange(outer, dtype=jnp.int32)
    fine = jnp.arange(inner, dtype=jnp.int32)
    scale = 2.0 * math.pi / cycle_size
    theta_a = (wave_order[:, None] * coarse[None, :] % cycle_size).astype(jnp.float32) * scale
    theta_b = (wave_order[:, None] * fine[None, :] % cycle_size).astype(jnp.float32) * scale
    cos_a = jnp.cos(theta_a)[:, :, None]
    sin_a = jnp.sin(theta_a)[:, :, None]
    cos_b = jnp.cos(theta_b)[:, None, :]
    sin_b = jnp.sin(theta_b)[:, None, :]
    factor = jnp.where(wave_order == 0, 1.0, 2.0).astype(jnp.float32)[:, None, None]
    real = factor * (cos_a * cos_b - sin_a * sin_b)
    imag = -factor * (sin_a * cos_b + cos_a * sin_b)
    count = wave_order.shape[0]
    return jnp.stack([real.reshape(count, lon_count), imag.reshape(count, lon_count)]).astype(
        jnp.bfloat16
    )


def shift_weight(offsets, frac, shift):
    zeros = jnp.zeros_like(frac)
    lower = jnp.where(offsets == shift, 1.0 - frac, zeros)
    higher = jnp.where(offsets == shift - 1, frac, zeros)
    return lower + higher


def line_gather(block, axis):
    count = lax.axis_size(axis)
    here = lax.axis_index(axis)
    slots = jnp.zeros((count + 1,) + block.shape, block.dtype)
    slots = lax.dynamic_update_index_in_dim(slots, block, here, 0)
    right = block
    left = block
    for hop in range(1, count):
        right = lax.ppermute(right, axis, [(i, i + 1) for i in range(hop - 1, count - 1)])
        left = lax.ppermute(left, axis, [(i, i - 1) for i in range(1, count - hop + 1)])
        slots = lax.dynamic_update_index_in_dim(
            slots, right, jnp.where(here >= hop, here - hop, count), 0
        )
        slots = lax.dynamic_update_index_in_dim(
            slots, left, jnp.where(here + hop <= count - 1, here + hop, count), 0
        )
    return slots[:count]


def _block_size(count):
    for size in (8, 5, 4, 2, 1):
        if count % size == 0:
            return size
    return 1


def legendre_kernel(ids_ref, coef_ref, leg_ref, out_ref):
    step = pl.program_id(0)
    block = coef_ref.shape[0]
    bands = out_ref.shape[1]
    rows = out_ref.shape[3]
    degree_count = coef_ref.shape[2]
    degree = lax.broadcasted_iota(jnp.int32, (1, degree_count), 1)
    for w in range(block):
        wave = ids_ref[step * block + w]
        coef = coef_ref[w]
        kept = jnp.where(degree >= wave, coef, jnp.zeros((), coef.dtype))
        prod = lax.dot_general(
            leg_ref[w], kept, (((1,), (1,)), ((), ())), preferred_element_type=jnp.float32
        )
        out_ref[0, :, w, :, :] = prod.astype(out_ref.dtype).reshape(bands, rows, prod.shape[1])


def legendre_transform(local_ids, coef, leg, bands, chunks):
    local_waves, width, degree_count = coef.shape
    lats = leg.shape[1]
    rows = lats // bands
    chunk_waves = local_waves // chunks
    block = _block_size(chunk_waves)
    per_chunk = chunk_waves // block
    return pl.pallas_call(
        legendre_kernel,
        out_shape=jax.ShapeDtypeStruct((chunks, bands, chunk_waves, rows, width), jnp.bfloat16),
        grid_spec=pltpu.PrefetchScalarGridSpec(
            num_scalar_prefetch=1,
            grid=(local_waves // block,),
            in_specs=[
                pl.BlockSpec((block, width, degree_count), lambda i, ids: (i, 0, 0)),
                pl.BlockSpec((block, lats, degree_count), lambda i, ids: (i, 0, 0)),
            ],
            out_specs=pl.BlockSpec(
                (1, bands, block, rows, width),
                lambda i, ids: (i // per_chunk, 0, i % per_chunk, 0, 0),
            ),
        ),
    )(local_ids, coef, leg)


def per_device(spec_coef, legendre, wave_ids, dep_drow, dep_dlon, dep_frac):
    lat_count = lax.axis_size("lat")
    lon_parts = lax.axis_size("lon")
    local_waves = spec_coef.shape[0]
    level_fields = spec_coef.shape[2]
    degree_count = spec_coef.shape[3]
    all_waves = wave_ids.shape[0]
    row_count = dep_drow.shape[0]
    sector_width = dep_drow.shape[1]
    cycle_size = sector_width * lon_parts
    device = lax.axis_index("lat") * lon_parts + lax.axis_index("lon")
    local_ids = lax.dynamic_slice_in_dim(wave_ids, device * local_waves, local_waves)
    coef = spec_coef.reshape(local_waves, 2 * level_fields, degree_count)
    chunks = 2 if local_waves % 2 == 0 else 1
    chunk_waves = local_waves // chunks
    fourier = legendre_transform(local_ids, coef, legendre, lat_count, chunks)
    lon_start = lax.axis_index("lon") * sector_width
    by_chunk = wave_ids.reshape(lat_count, lon_parts, chunks, chunk_waves)
    total = None
    for c in range(chunks):
        moved = lax.all_to_all(fourier[c], "lat", split_axis=0, concat_axis=0, tiled=True)
        gathered = line_gather(moved, "lon")
        gathered = gathered.reshape(lon_parts * lat_count * chunk_waves, row_count, 2, level_fields)
        wave_order = by_chunk[:, :, c, :].transpose(1, 0, 2).reshape(-1)
        table = wave_table(wave_order, lon_start, sector_width, cycle_size)
        part = jnp.einsum("mprq,rmx->qpx", gathered, table, preferred_element_type=jnp.float32)
        total = part if total is None else total + part
    grid = total.astype(jnp.bfloat16)
    margin = REACH + 1
    tall = padded_2(grid, (("lat", 1),), margin, False)
    padded = padded_2(tall, (("lon", 2),), margin, True)
    frac_row = dep_frac[0]
    frac_col = dep_frac[1]
    col_weights = [shift_weight(dep_dlon, frac_col, shift) for shift in range(-REACH, REACH + 2)]
    total = jnp.zeros((level_fields, row_count, sector_width), jnp.float32)
    for row_shift in range(-REACH, REACH + 2):
        band = padded[:, margin + row_shift : margin + row_shift + row_count, :]
        along = jnp.zeros((level_fields, row_count, sector_width), jnp.float32)
        for place, col_shift in enumerate(range(-REACH, REACH + 2)):
            window = band[:, :, margin + col_shift : margin + col_shift + sector_width].astype(
                jnp.float32
            )
            along = along + col_weights[place][None] * window
        total = total + shift_weight(dep_drow, frac_row, row_shift)[None] * along
    return (grid, total.astype(jnp.bfloat16))


def solution(mesh):
    in_specs = (
        P(("lat", "lon"), None, None, None),
        P(("lat", "lon"), None, None),
        P(),
        P("lat", "lon"),
        P("lat", "lon"),
        P(None, "lat", "lon"),
    )
    out_specs = (P(None, "lat", "lon"), P(None, "lat", "lon"))
    return jax.shard_map(
        per_device, mesh=mesh, in_specs=in_specs, out_specs=out_specs, check_vma=False
    )
```

```python
import math

import jax
import jax.numpy as jnp
from jax import lax
from jax.experimental import pallas as pl
from jax.experimental.pallas import tpu as pltpu
from jax.sharding import PartitionSpec as P

REACH = 1


def padded_2(cells, sides, width, closed):
    for axis, dim in sides:
        count = lax.axis_size(axis)
        ends = count if closed else count - 1
        head = lax.slice_in_dim(cells, 0, width, axis=dim)
        tail = lax.slice_in_dim(cells, cells.shape[dim] - width, cells.shape[dim], axis=dim)
        cells = jnp.concatenate(
            [
                lax.ppermute(tail, axis, [(i, (i + 1) % count) for i in range(ends)]),
                cells,
                lax.ppermute(head, axis, [((i + 1) % count, i) for i in range(ends)]),
            ],
            axis=dim,
        )
    return cells


def wave_table(wave_order, lon_start, lon_count, cycle_size):
    inner = 128 if lon_count % 128 == 0 else lon_count
    outer = lon_count // inner
    coarse = lon_start + inner * jnp.arange(outer, dtype=jnp.int32)
    fine = jnp.arange(inner, dtype=jnp.int32)
    scale = 2.0 * math.pi / cycle_size
    theta_a = (wave_order[:, None] * coarse[None, :] % cycle_size).astype(jnp.float32) * scale
    theta_b = (wave_order[:, None] * fine[None, :] % cycle_size).astype(jnp.float32) * scale
    cos_a = jnp.cos(theta_a)[:, :, None]
    sin_a = jnp.sin(theta_a)[:, :, None]
    cos_b = jnp.cos(theta_b)[:, None, :]
    sin_b = jnp.sin(theta_b)[:, None, :]
    factor = jnp.where(wave_order == 0, 1.0, 2.0).astype(jnp.float32)[:, None, None]
    real = factor * (cos_a * cos_b - sin_a * sin_b)
    imag = -factor * (sin_a * cos_b + cos_a * sin_b)
    count = wave_order.shape[0]
    return jnp.stack([real.reshape(count, lon_count), imag.reshape(count, lon_count)]).astype(
        jnp.bfloat16
    )


def shift_weight(offsets, frac, shift):
    zeros = jnp.zeros_like(frac)
    lower = jnp.where(offsets == shift, 1.0 - frac, zeros)
    higher = jnp.where(offsets == shift - 1, frac, zeros)
    return lower + higher


def _block_size(count):
    for size in (8, 5, 4, 2, 1):
        if count % size == 0:
            return size
    return 1


def legendre_kernel(ids_ref, coef_ref, leg_ref, out_ref):
    step = pl.program_id(0)
    block = coef_ref.shape[0]
    bands = out_ref.shape[1]
    rows = out_ref.shape[3]
    degree_count = coef_ref.shape[2]
    degree = lax.broadcasted_iota(jnp.int32, (1, degree_count), 1)
    for w in range(block):
        wave = ids_ref[step * block + w]
        coef = coef_ref[w]
        kept = jnp.where(degree >= wave, coef, jnp.zeros((), coef.dtype))
        prod = lax.dot_general(
            leg_ref[w], kept, (((1,), (1,)), ((), ())), preferred_element_type=jnp.float32
        )
        out_ref[0, :, w, :, :] = prod.astype(out_ref.dtype).reshape(bands, rows, prod.shape[1])


def legendre_transform(local_ids, coef, leg, bands, chunks, chunk):
    local_waves, width, degree_count = coef.shape
    lats = leg.shape[1]
    rows = lats // bands
    chunk_waves = local_waves // chunks
    block = _block_size(chunk_waves)
    steps = chunk_waves // block
    first = chunk * steps
    ids = lax.dynamic_slice_in_dim(local_ids, chunk * chunk_waves, chunk_waves)
    return pl.pallas_call(
        legendre_kernel,
        out_shape=jax.ShapeDtypeStruct((1, bands, chunk_waves, rows, width), jnp.bfloat16),
        grid_spec=pltpu.PrefetchScalarGridSpec(
            num_scalar_prefetch=1,
            grid=(steps,),
            in_specs=[
                pl.BlockSpec((block, width, degree_count), lambda i, ids: (first + i, 0, 0)),
                pl.BlockSpec((block, lats, degree_count), lambda i, ids: (first + i, 0, 0)),
            ],
            out_specs=pl.BlockSpec((1, bands, block, rows, width), lambda i, ids: (0, 0, i, 0, 0)),
        ),
    )(ids, coef, leg)[0]


def per_device(spec_coef, legendre, wave_ids, dep_drow, dep_dlon, dep_frac):
    lat_count = lax.axis_size("lat")
    lon_parts = lax.axis_size("lon")
    local_waves = spec_coef.shape[0]
    level_fields = spec_coef.shape[2]
    degree_count = spec_coef.shape[3]
    all_waves = wave_ids.shape[0]
    row_count = dep_drow.shape[0]
    sector_width = dep_drow.shape[1]
    cycle_size = sector_width * lon_parts
    device = lax.axis_index("lat") * lon_parts + lax.axis_index("lon")
    local_ids = lax.dynamic_slice_in_dim(wave_ids, device * local_waves, local_waves)
    coef = spec_coef.reshape(local_waves, 2 * level_fields, degree_count)
    chunks = next(c for c in (4, 2, 1) if local_waves % c == 0)
    chunk_waves = local_waves // chunks
    lon_start = lax.axis_index("lon") * sector_width
    by_chunk = wave_ids.reshape(lat_count, lon_parts, chunks, chunk_waves).transpose(2, 1, 0, 3)
    table = wave_table(by_chunk.reshape(all_waves), lon_start, sector_width, cycle_size)
    span = all_waves // chunks
    total = None
    for c in range(chunks):
        fourier = legendre_transform(local_ids, coef, legendre, lat_count, chunks, c)
        moved = lax.all_to_all(fourier, "lat", split_axis=0, concat_axis=0, tiled=True)
        gathered = lax.all_gather(moved, "lon", axis=0, tiled=True)
        gathered = gathered.reshape(lon_parts * lat_count * chunk_waves, row_count, 2, level_fields)
        part = jnp.einsum(
            "mprq,rmx->qpx",
            gathered,
            table[:, c * span : (c + 1) * span],
            preferred_element_type=jnp.float32,
        )
        total = part if total is None else total + part
    grid = total.astype(jnp.bfloat16)
    margin = REACH + 1
    tall = padded_2(grid, (("lat", 1),), margin, False)
    padded = padded_2(tall, (("lon", 2),), margin, True)
    frac_row = dep_frac[0]
    frac_col = dep_frac[1]
    col_weights = [shift_weight(dep_dlon, frac_col, shift) for shift in range(-REACH, REACH + 2)]
    total = jnp.zeros((level_fields, row_count, sector_width), jnp.float32)
    for row_shift in range(-REACH, REACH + 2):
        band = padded[:, margin + row_shift : margin + row_shift + row_count, :]
        along = jnp.zeros((level_fields, row_count, sector_width), jnp.float32)
        for place, col_shift in enumerate(range(-REACH, REACH + 2)):
            window = band[:, :, margin + col_shift : margin + col_shift + sector_width].astype(
                jnp.float32
            )
            along = along + col_weights[place][None] * window
        total = total + shift_weight(dep_drow, frac_row, row_shift)[None] * along
    return (grid, total.astype(jnp.bfloat16))


def solution(mesh):
    in_specs = (
        P(("lat", "lon"), None, None, None),
        P(("lat", "lon"), None, None),
        P(),
        P("lat", "lon"),
        P("lat", "lon"),
        P(None, "lat", "lon"),
    )
    out_specs = (P(None, "lat", "lon"), P(None, "lat", "lon"))
    return jax.shard_map(
        per_device, mesh=mesh, in_specs=in_specs, out_specs=out_specs, check_vma=False
    )
```

```python
import math

import jax
import jax.numpy as jnp
from jax import lax
from jax.experimental import pallas as pl
from jax.experimental.pallas import tpu as pltpu
from jax.sharding import PartitionSpec as P

REACH = 1


def wave_table(wave_order, lon_start, lon_count, cycle_size):
    inner = 128 if lon_count % 128 == 0 else lon_count
    outer = lon_count // inner
    coarse = lon_start + inner * jnp.arange(outer, dtype=jnp.int32)
    fine = jnp.arange(inner, dtype=jnp.int32)
    scale = 2.0 * math.pi / cycle_size
    theta_a = (wave_order[:, None] * coarse[None, :] % cycle_size).astype(jnp.float32) * scale
    theta_b = (wave_order[:, None] * fine[None, :] % cycle_size).astype(jnp.float32) * scale
    cos_a = jnp.cos(theta_a)[:, :, None]
    sin_a = jnp.sin(theta_a)[:, :, None]
    cos_b = jnp.cos(theta_b)[:, None, :]
    sin_b = jnp.sin(theta_b)[:, None, :]
    factor = jnp.where(wave_order == 0, 1.0, 2.0).astype(jnp.float32)[:, None, None]
    real = factor * (cos_a * cos_b - sin_a * sin_b)
    imag = -factor * (sin_a * cos_b + cos_a * sin_b)
    count = wave_order.shape[0]
    return jnp.stack([real.reshape(count, lon_count), imag.reshape(count, lon_count)]).astype(
        jnp.bfloat16
    )


def edge_table(wave_order, columns, cycle_size):
    phase_index = wave_order[:, None] * (columns[None, :] % cycle_size) % cycle_size
    theta = phase_index.astype(jnp.float32) * (2.0 * math.pi / cycle_size)
    factor = jnp.where(wave_order == 0, 1.0, 2.0).astype(jnp.float32)[:, None]
    return jnp.stack([factor * jnp.cos(theta), -factor * jnp.sin(theta)]).astype(jnp.bfloat16)


def shift_weight(offsets, frac, shift):
    zeros = jnp.zeros_like(frac)
    lower = jnp.where(offsets == shift, 1.0 - frac, zeros)
    higher = jnp.where(offsets == shift - 1, frac, zeros)
    return lower + higher


def _block_size(count):
    for size in (8, 5, 4, 2, 1):
        if count % size == 0:
            return size
    return 1


def legendre_kernel(ids_ref, coef_ref, leg_ref, out_ref):
    step = pl.program_id(0)
    block = coef_ref.shape[0]
    bands = out_ref.shape[1]
    rows = out_ref.shape[3]
    degree_count = coef_ref.shape[2]
    degree = lax.broadcasted_iota(jnp.int32, (1, degree_count), 1)
    for w in range(block):
        wave = ids_ref[step * block + w]
        coef = coef_ref[w]
        kept = jnp.where(degree >= wave, coef, jnp.zeros((), coef.dtype))
        prod = lax.dot_general(
            leg_ref[w], kept, (((1,), (1,)), ((), ())), preferred_element_type=jnp.float32
        )
        out_ref[0, :, w, :, :] = prod.astype(out_ref.dtype).reshape(bands, rows, prod.shape[1])


def legendre_transform(local_ids, coef, leg, bands, chunks):
    local_waves, width, degree_count = coef.shape
    lats = leg.shape[1]
    rows = lats // bands
    chunk_waves = local_waves // chunks
    block = _block_size(chunk_waves)
    per_chunk = chunk_waves // block
    return pl.pallas_call(
        legendre_kernel,
        out_shape=jax.ShapeDtypeStruct((chunks, bands, chunk_waves, rows, width), jnp.bfloat16),
        grid_spec=pltpu.PrefetchScalarGridSpec(
            num_scalar_prefetch=1,
            grid=(local_waves // block,),
            in_specs=[
                pl.BlockSpec((block, width, degree_count), lambda i, ids: (i, 0, 0)),
                pl.BlockSpec((block, lats, degree_count), lambda i, ids: (i, 0, 0)),
            ],
            out_specs=pl.BlockSpec(
                (1, bands, block, rows, width),
                lambda i, ids: (i // per_chunk, 0, i % per_chunk, 0, 0),
            ),
        ),
    )(local_ids, coef, leg)


def per_device(spec_coef, legendre, wave_ids, dep_drow, dep_dlon, dep_frac):
    lat_count = lax.axis_size("lat")
    lon_parts = lax.axis_size("lon")
    local_waves = spec_coef.shape[0]
    level_fields = spec_coef.shape[2]
    degree_count = spec_coef.shape[3]
    all_waves = wave_ids.shape[0]
    row_count = dep_drow.shape[0]
    sector_width = dep_drow.shape[1]
    cycle_size = sector_width * lon_parts
    device = lax.axis_index("lat") * lon_parts + lax.axis_index("lon")
    local_ids = lax.dynamic_slice_in_dim(wave_ids, device * local_waves, local_waves)
    coef = spec_coef.reshape(local_waves, 2 * level_fields, degree_count)
    chunks = 2 if local_waves % 2 == 0 else 1
    chunk_waves = local_waves // chunks
    fourier = legendre_transform(local_ids, coef, legendre, lat_count, chunks)
    lon_start = lax.axis_index("lon") * sector_width
    above = REACH
    below = REACH + 1
    left = REACH
    right = REACH + 1
    edge_cols = lon_start + jnp.concatenate(
        [jnp.arange(-left, 0, dtype=jnp.int32), sector_width + jnp.arange(right, dtype=jnp.int32)]
    )
    by_chunk = wave_ids.reshape(lat_count, lon_parts, chunks, chunk_waves)
    down_pairs = [(i, i + 1) for i in range(lat_count - 1)]
    up_pairs = [(i + 1, i) for i in range(lat_count - 1)]
    main = None
    for c in range(chunks):
        moved = lax.all_to_all(fourier[c], "lat", split_axis=0, concat_axis=0, tiled=True)
        gathered = lax.all_gather(moved, "lon", axis=0, tiled=True)
        waves = lon_parts * lat_count * chunk_waves
        gathered = gathered.reshape(waves, row_count, 2 * level_fields)
        halo = jnp.concatenate(
            [
                lax.ppermute(gathered[:, row_count - above :], "lat", down_pairs),
                lax.ppermute(gathered[:, :below], "lat", up_pairs),
            ],
            axis=1,
        )
        wave_order = by_chunk[:, :, c, :].transpose(1, 0, 2).reshape(-1)
        table = wave_table(wave_order, lon_start, sector_width, cycle_size)
        side = edge_table(wave_order, edge_cols, cycle_size)
        inner = gathered.reshape(waves, row_count, 2, level_fields)
        outer = halo.reshape(waves, above + below, 2, level_fields)
        parts = [
            jnp.einsum("mprq,rmx->qpx", a, b, preferred_element_type=jnp.float32)
            for a, b in ((inner, table), (inner, side), (outer, table), (outer, side))
        ]
        main = parts if main is None else [x + y for x, y in zip(main, parts)]
    center, sides, rims, corners = [x.astype(jnp.bfloat16) for x in main]
    grid = center
    wide_mid = jnp.concatenate([sides[:, :, :left], center, sides[:, :, left:]], axis=2)
    wide_rim = jnp.concatenate([corners[:, :, :left], rims, corners[:, :, left:]], axis=2)
    padded = jnp.concatenate([wide_rim[:, :above], wide_mid, wide_rim[:, above:]], axis=1)
    frac_row = dep_frac[0]
    frac_col = dep_frac[1]
    col_weights = [shift_weight(dep_dlon, frac_col, shift) for shift in range(-REACH, REACH + 2)]
    total = jnp.zeros((level_fields, row_count, sector_width), jnp.float32)
    for row_shift in range(-REACH, REACH + 2):
        band = padded[:, above + row_shift : above + row_shift + row_count, :]
        along = jnp.zeros((level_fields, row_count, sector_width), jnp.float32)
        for place, col_shift in enumerate(range(-REACH, REACH + 2)):
            window = band[:, :, left + col_shift : left + col_shift + sector_width].astype(
                jnp.float32
            )
            along = along + col_weights[place][None] * window
        total = total + shift_weight(dep_drow, frac_row, row_shift)[None] * along
    return (grid, total.astype(jnp.bfloat16))


def solution(mesh):
    in_specs = (
        P(("lat", "lon"), None, None, None),
        P(("lat", "lon"), None, None),
        P(),
        P("lat", "lon"),
        P("lat", "lon"),
        P(None, "lat", "lon"),
    )
    out_specs = (P(None, "lat", "lon"), P(None, "lat", "lon"))
    return jax.shard_map(
        per_device, mesh=mesh, in_specs=in_specs, out_specs=out_specs, check_vma=False
    )
```

```python
import math

import jax
import jax.numpy as jnp
from jax import lax
from jax.experimental import pallas as pl
from jax.experimental.pallas import tpu as pltpu
from jax.sharding import PartitionSpec as P

REACH = 1


def halo_pad(cells, before, after):
    rows_n = lax.axis_size("lat")
    cols_n = lax.axis_size("lon")
    _, rows, cols = cells.shape
    top = cells[:, rows - before :]
    bottom = cells[:, :after]
    down = [(i, i + 1) for i in range(rows_n - 1)]
    up = [(i + 1, i) for i in range(rows_n - 1)]
    east = [(j, (j + 1) % cols_n) for j in range(cols_n)]
    west = [((j + 1) % cols_n, j) for j in range(cols_n)]

    def both(row_pairs, col_pairs):
        return [
            (a * cols_n + b, c * cols_n + d) for a, c in row_pairs for b, d in col_pairs
        ]

    def corner(block, row_pairs, col_pairs):
        return lax.ppermute(block, ("lat", "lon"), both(row_pairs, col_pairs))

    above = lax.ppermute(top, "lat", down)
    below = lax.ppermute(bottom, "lat", up)
    west_cells = lax.ppermute(cells[:, :, cols - before :], "lon", east)
    east_cells = lax.ppermute(cells[:, :, :after], "lon", west)
    above_west = corner(top[:, :, cols - before :], down, east)
    above_east = corner(top[:, :, :after], down, west)
    below_west = corner(bottom[:, :, cols - before :], up, east)
    below_east = corner(bottom[:, :, :after], up, west)
    return jnp.concatenate(
        [
            jnp.concatenate([above_west, above, above_east], axis=2),
            jnp.concatenate([west_cells, cells, east_cells], axis=2),
            jnp.concatenate([below_west, below, below_east], axis=2),
        ],
        axis=1,
    )


def wave_table(wave_order, lon_start, lon_count, cycle_size):
    inner = 128 if lon_count % 128 == 0 else lon_count
    outer = lon_count // inner
    coarse = lon_start + inner * jnp.arange(outer, dtype=jnp.int32)
    fine = jnp.arange(inner, dtype=jnp.int32)
    scale = 2.0 * math.pi / cycle_size
    theta_a = (wave_order[:, None] * coarse[None, :] % cycle_size).astype(jnp.float32) * scale
    theta_b = (wave_order[:, None] * fine[None, :] % cycle_size).astype(jnp.float32) * scale
    cos_a = jnp.cos(theta_a)[:, :, None]
    sin_a = jnp.sin(theta_a)[:, :, None]
    cos_b = jnp.cos(theta_b)[:, None, :]
    sin_b = jnp.sin(theta_b)[:, None, :]
    factor = jnp.where(wave_order == 0, 1.0, 2.0).astype(jnp.float32)[:, None, None]
    real = factor * (cos_a * cos_b - sin_a * sin_b)
    imag = -factor * (sin_a * cos_b + cos_a * sin_b)
    count = wave_order.shape[0]
    return jnp.stack([real.reshape(count, lon_count), imag.reshape(count, lon_count)]).astype(
        jnp.bfloat16
    )


def shift_weight(offsets, frac, shift):
    zeros = jnp.zeros_like(frac)
    lower = jnp.where(offsets == shift, 1.0 - frac, zeros)
    higher = jnp.where(offsets == shift - 1, frac, zeros)
    return lower + higher


def _block_size(count):
    for size in (8, 5, 4, 2, 1):
        if count % size == 0:
            return size
    return 1


def legendre_kernel(ids_ref, coef_ref, leg_ref, out_ref):
    step = pl.program_id(0)
    block = coef_ref.shape[0]
    bands = out_ref.shape[1]
    rows = out_ref.shape[3]
    degree_count = coef_ref.shape[2]
    degree = lax.broadcasted_iota(jnp.int32, (1, degree_count), 1)
    for w in range(block):
        wave = ids_ref[step * block + w]
        coef = coef_ref[w]
        kept = jnp.where(degree >= wave, coef, jnp.zeros((), coef.dtype))
        prod = lax.dot_general(
            leg_ref[w], kept, (((1,), (1,)), ((), ())), preferred_element_type=jnp.float32
        )
        out_ref[0, :, w, :, :] = prod.astype(out_ref.dtype).reshape(bands, rows, prod.shape[1])


def legendre_transform(local_ids, coef, leg, bands, chunks, chunk):
    local_waves, width, degree_count = coef.shape
    lats = leg.shape[1]
    rows = lats // bands
    chunk_waves = local_waves // chunks
    block = _block_size(chunk_waves)
    steps = chunk_waves // block
    first = chunk * steps
    ids = lax.dynamic_slice_in_dim(local_ids, chunk * chunk_waves, chunk_waves)
    return pl.pallas_call(
        legendre_kernel,
        out_shape=jax.ShapeDtypeStruct((1, bands, chunk_waves, rows, width), jnp.bfloat16),
        grid_spec=pltpu.PrefetchScalarGridSpec(
            num_scalar_prefetch=1,
            grid=(steps,),
            in_specs=[
                pl.BlockSpec((block, width, degree_count), lambda i, ids: (first + i, 0, 0)),
                pl.BlockSpec((block, lats, degree_count), lambda i, ids: (first + i, 0, 0)),
            ],
            out_specs=pl.BlockSpec((1, bands, block, rows, width), lambda i, ids: (0, 0, i, 0, 0)),
        ),
    )(ids, coef, leg)[0]


def per_device(spec_coef, legendre, wave_ids, dep_drow, dep_dlon, dep_frac):
    lat_count = lax.axis_size("lat")
    lon_parts = lax.axis_size("lon")
    local_waves = spec_coef.shape[0]
    level_fields = spec_coef.shape[2]
    degree_count = spec_coef.shape[3]
    all_waves = wave_ids.shape[0]
    row_count = dep_drow.shape[0]
    sector_width = dep_drow.shape[1]
    cycle_size = sector_width * lon_parts
    device = lax.axis_index("lat") * lon_parts + lax.axis_index("lon")
    local_ids = lax.dynamic_slice_in_dim(wave_ids, device * local_waves, local_waves)
    coef = spec_coef.reshape(local_waves, 2 * level_fields, degree_count)
    chunks = 2 if local_waves % 2 == 0 else 1
    chunk_waves = local_waves // chunks
    lon_start = lax.axis_index("lon") * sector_width
    by_chunk = wave_ids.reshape(lat_count, lon_parts, chunks, chunk_waves)
    total = None
    for c in range(chunks):
        fourier = legendre_transform(local_ids, coef, legendre, lat_count, chunks, c)
        moved = lax.all_to_all(fourier, "lat", split_axis=0, concat_axis=0, tiled=True)
        gathered = lax.all_gather(moved, "lon", axis=0, tiled=True)
        gathered = gathered.reshape(lon_parts * lat_count * chunk_waves, row_count, 2, level_fields)
        wave_order = by_chunk[:, :, c, :].transpose(1, 0, 2).reshape(-1)
        table = wave_table(wave_order, lon_start, sector_width, cycle_size)
        part = jnp.einsum("mprq,rmx->qpx", gathered, table, preferred_element_type=jnp.float32)
        total = part if total is None else total + part
    grid = total.astype(jnp.bfloat16)
    before = REACH
    padded = halo_pad(grid, before, REACH + 1)
    frac_row = dep_frac[0]
    frac_col = dep_frac[1]
    col_weights = [shift_weight(dep_dlon, frac_col, shift) for shift in range(-REACH, REACH + 2)]
    total = jnp.zeros((level_fields, row_count, sector_width), jnp.float32)
    for row_shift in range(-REACH, REACH + 2):
        band = padded[:, before + row_shift : before + row_shift + row_count, :]
        along = jnp.zeros((level_fields, row_count, sector_width), jnp.float32)
        for place, col_shift in enumerate(range(-REACH, REACH + 2)):
            window = band[:, :, before + col_shift : before + col_shift + sector_width].astype(
                jnp.float32
            )
            along = along + col_weights[place][None] * window
        total = total + shift_weight(dep_drow, frac_row, row_shift)[None] * along
    return (grid, total.astype(jnp.bfloat16))


def solution(mesh):
    in_specs = (
        P(("lat", "lon"), None, None, None),
        P(("lat", "lon"), None, None),
        P(),
        P("lat", "lon"),
        P("lat", "lon"),
        P(None, "lat", "lon"),
    )
    out_specs = (P(None, "lat", "lon"), P(None, "lat", "lon"))
    return jax.shard_map(
        per_device, mesh=mesh, in_specs=in_specs, out_specs=out_specs, check_vma=False
    )
```

```python
import math

import jax
import jax.numpy as jnp
from jax import lax
from jax.experimental import pallas as pl
from jax.experimental.pallas import tpu as pltpu
from jax.sharding import PartitionSpec as P

REACH = 1


def padded_2(cells, sides, width, closed):
    for axis, dim in sides:
        count = lax.axis_size(axis)
        ends = count if closed else count - 1
        head = lax.slice_in_dim(cells, 0, width, axis=dim)
        tail = lax.slice_in_dim(cells, cells.shape[dim] - width, cells.shape[dim], axis=dim)
        cells = jnp.concatenate(
            [
                lax.ppermute(tail, axis, [(i, (i + 1) % count) for i in range(ends)]),
                cells,
                lax.ppermute(head, axis, [((i + 1) % count, i) for i in range(ends)]),
            ],
            axis=dim,
        )
    return cells


def wave_table(wave_order, lon_start, lon_count, cycle_size):
    inner = 128 if lon_count % 128 == 0 else lon_count
    outer = lon_count // inner
    coarse = lon_start + inner * jnp.arange(outer, dtype=jnp.int32)
    fine = jnp.arange(inner, dtype=jnp.int32)
    scale = 2.0 * math.pi / cycle_size
    theta_a = (wave_order[:, None] * coarse[None, :] % cycle_size).astype(jnp.float32) * scale
    theta_b = (wave_order[:, None] * fine[None, :] % cycle_size).astype(jnp.float32) * scale
    cos_a = jnp.cos(theta_a)[:, :, None]
    sin_a = jnp.sin(theta_a)[:, :, None]
    cos_b = jnp.cos(theta_b)[:, None, :]
    sin_b = jnp.sin(theta_b)[:, None, :]
    factor = jnp.where(wave_order == 0, 1.0, 2.0).astype(jnp.float32)[:, None, None]
    real = factor * (cos_a * cos_b - sin_a * sin_b)
    imag = -factor * (sin_a * cos_b + cos_a * sin_b)
    count = wave_order.shape[0]
    return jnp.stack([real.reshape(count, lon_count), imag.reshape(count, lon_count)]).astype(
        jnp.bfloat16
    )


def shift_weight(offsets, frac, shift):
    zeros = jnp.zeros_like(frac)
    lower = jnp.where(offsets == shift, 1.0 - frac, zeros)
    higher = jnp.where(offsets == shift - 1, frac, zeros)
    return lower + higher


def _block_size(count):
    for size in (8, 5, 4, 2, 1):
        if count % size == 0:
            return size
    return 1


def legendre_kernel(ids_ref, coef_ref, leg_ref, out_ref):
    step = pl.program_id(0)
    block = coef_ref.shape[0]
    bands = out_ref.shape[1]
    rows = out_ref.shape[3]
    degree_count = coef_ref.shape[2]
    degree = lax.broadcasted_iota(jnp.int32, (1, degree_count), 1)
    for w in range(block):
        wave = ids_ref[step * block + w]
        coef = coef_ref[w]
        kept = jnp.where(degree >= wave, coef, jnp.zeros((), coef.dtype))
        prod = lax.dot_general(
            leg_ref[w], kept, (((1,), (1,)), ((), ())), preferred_element_type=jnp.float32
        )
        out_ref[0, :, w, :, :] = prod.astype(out_ref.dtype).reshape(bands, rows, prod.shape[1])


def legendre_transform(local_ids, coef, leg, bands, chunks, chunk):
    local_waves, width, degree_count = coef.shape
    lats = leg.shape[1]
    rows = lats // bands
    chunk_waves = local_waves // chunks
    block = _block_size(chunk_waves)
    steps = chunk_waves // block
    first = chunk * steps
    ids = lax.dynamic_slice_in_dim(local_ids, chunk * chunk_waves, chunk_waves)
    return pl.pallas_call(
        legendre_kernel,
        out_shape=jax.ShapeDtypeStruct((1, bands, chunk_waves, rows, width), jnp.bfloat16),
        grid_spec=pltpu.PrefetchScalarGridSpec(
            num_scalar_prefetch=1,
            grid=(steps,),
            in_specs=[
                pl.BlockSpec((block, width, degree_count), lambda i, ids: (first + i, 0, 0)),
                pl.BlockSpec((block, lats, degree_count), lambda i, ids: (first + i, 0, 0)),
            ],
            out_specs=pl.BlockSpec((1, bands, block, rows, width), lambda i, ids: (0, 0, i, 0, 0)),
        ),
    )(ids, coef, leg)[0]


def per_device(spec_coef, legendre, wave_ids, dep_drow, dep_dlon, dep_frac):
    lat_count = lax.axis_size("lat")
    lon_parts = lax.axis_size("lon")
    local_waves = spec_coef.shape[0]
    level_fields = spec_coef.shape[2]
    degree_count = spec_coef.shape[3]
    all_waves = wave_ids.shape[0]
    row_count = dep_drow.shape[0]
    sector_width = dep_drow.shape[1]
    cycle_size = sector_width * lon_parts
    device = lax.axis_index("lat") * lon_parts + lax.axis_index("lon")
    local_ids = lax.dynamic_slice_in_dim(wave_ids, device * local_waves, local_waves)
    coef = spec_coef.reshape(local_waves, 2 * level_fields, degree_count)
    chunks = 2 if local_waves % 2 == 0 else 1
    chunk_waves = local_waves // chunks
    lon_start = lax.axis_index("lon") * sector_width
    by_chunk = wave_ids.reshape(lat_count, lon_parts, chunks, chunk_waves)
    total = None
    for c in range(chunks):
        fourier = legendre_transform(local_ids, coef, legendre, lat_count, chunks, c)
        moved = lax.all_to_all(fourier, "lat", split_axis=0, concat_axis=0, tiled=True)
        gathered = lax.all_gather(moved, "lon", axis=0, tiled=True)
        gathered = gathered.reshape(lon_parts * lat_count * chunk_waves, row_count, 2, level_fields)
        wave_order = by_chunk[:, :, c, :].transpose(1, 0, 2).reshape(-1)
        table = wave_table(wave_order, lon_start, sector_width, cycle_size)
        part = jnp.einsum("mprq,rmx->qpx", gathered, table, preferred_element_type=jnp.float32)
        total = part if total is None else total + part
    grid = total.astype(jnp.bfloat16)
    margin = REACH + 1
    tall = padded_2(grid, (("lat", 1),), margin, False)
    padded = padded_2(tall, (("lon", 2),), margin, True)
    frac_row = dep_frac[0]
    frac_col = dep_frac[1]
    col_weights = [shift_weight(dep_dlon, frac_col, shift) for shift in range(-REACH, REACH + 2)]
    total = jnp.zeros((level_fields, row_count, sector_width), jnp.float32)
    for row_shift in range(-REACH, REACH + 2):
        band = padded[:, margin + row_shift : margin + row_shift + row_count, :]
        along = jnp.zeros((level_fields, row_count, sector_width), jnp.float32)
        for place, col_shift in enumerate(range(-REACH, REACH + 2)):
            window = band[:, :, margin + col_shift : margin + col_shift + sector_width].astype(
                jnp.float32
            )
            along = along + col_weights[place][None] * window
        total = total + shift_weight(dep_drow, frac_row, row_shift)[None] * along
    return (grid, total.astype(jnp.bfloat16))


def solution(mesh):
    in_specs = (
        P(("lat", "lon"), None, None, None),
        P(("lat", "lon"), None, None),
        P(),
        P("lat", "lon"),
        P("lat", "lon"),
        P(None, "lat", "lon"),
    )
    out_specs = (P(None, "lat", "lon"), P(None, "lat", "lon"))
    return jax.shard_map(
        per_device, mesh=mesh, in_specs=in_specs, out_specs=out_specs, check_vma=False
    )
```

```python
import math

import jax
import jax.numpy as jnp
from jax import lax
from jax.experimental import pallas as pl
from jax.experimental.pallas import tpu as pltpu
from jax.sharding import PartitionSpec as P

REACH = 1


def padded_2(cells, sides, width, closed):
    for axis, dim in sides:
        count = lax.axis_size(axis)
        ends = count if closed else count - 1
        head = lax.slice_in_dim(cells, 0, width, axis=dim)
        tail = lax.slice_in_dim(cells, cells.shape[dim] - width, cells.shape[dim], axis=dim)
        cells = jnp.concatenate(
            [
                lax.ppermute(tail, axis, [(i, (i + 1) % count) for i in range(ends)]),
                cells,
                lax.ppermute(head, axis, [((i + 1) % count, i) for i in range(ends)]),
            ],
            axis=dim,
        )
    return cells


def wave_table(wave_order, lon_start, lon_count, cycle_size):
    inner = 128 if lon_count % 128 == 0 else lon_count
    outer = lon_count // inner
    coarse = lon_start + inner * jnp.arange(outer, dtype=jnp.int32)
    fine = jnp.arange(inner, dtype=jnp.int32)
    scale = 2.0 * math.pi / cycle_size
    theta_a = (wave_order[:, None] * coarse[None, :] % cycle_size).astype(jnp.float32) * scale
    theta_b = (wave_order[:, None] * fine[None, :] % cycle_size).astype(jnp.float32) * scale
    cos_a = jnp.cos(theta_a)[:, :, None]
    sin_a = jnp.sin(theta_a)[:, :, None]
    cos_b = jnp.cos(theta_b)[:, None, :]
    sin_b = jnp.sin(theta_b)[:, None, :]
    factor = jnp.where(wave_order == 0, 1.0, 2.0).astype(jnp.float32)[:, None, None]
    real = factor * (cos_a * cos_b - sin_a * sin_b)
    imag = -factor * (sin_a * cos_b + cos_a * sin_b)
    count = wave_order.shape[0]
    return jnp.stack([real.reshape(count, lon_count), imag.reshape(count, lon_count)]).astype(
        jnp.bfloat16
    )


def edge_table(wave_order, columns, cycle_size):
    phase_index = wave_order[:, None] * (columns[None, :] % cycle_size) % cycle_size
    theta = phase_index.astype(jnp.float32) * (2.0 * math.pi / cycle_size)
    factor = jnp.where(wave_order == 0, 1.0, 2.0).astype(jnp.float32)[:, None]
    return jnp.stack([factor * jnp.cos(theta), -factor * jnp.sin(theta)]).astype(jnp.bfloat16)


def shift_weight(offsets, frac, shift):
    zeros = jnp.zeros_like(frac)
    lower = jnp.where(offsets == shift, 1.0 - frac, zeros)
    higher = jnp.where(offsets == shift - 1, frac, zeros)
    return lower + higher


def _block_size(count):
    for size in (8, 5, 4, 2, 1):
        if count % size == 0:
            return size
    return 1


def legendre_kernel(ids_ref, coef_ref, leg_ref, out_ref):
    step = pl.program_id(0)
    block = coef_ref.shape[0]
    bands = out_ref.shape[1]
    rows = out_ref.shape[3]
    degree_count = coef_ref.shape[2]
    degree = lax.broadcasted_iota(jnp.int32, (1, degree_count), 1)
    for w in range(block):
        wave = ids_ref[step * block + w]
        coef = coef_ref[w]
        kept = jnp.where(degree >= wave, coef, jnp.zeros((), coef.dtype))
        prod = lax.dot_general(
            leg_ref[w], kept, (((1,), (1,)), ((), ())), preferred_element_type=jnp.float32
        )
        out_ref[0, :, w, :, :] = prod.astype(out_ref.dtype).reshape(bands, rows, prod.shape[1])


def legendre_transform(local_ids, coef, leg, bands, chunks, chunk):
    local_waves, width, degree_count = coef.shape
    lats = leg.shape[1]
    rows = lats // bands
    chunk_waves = local_waves // chunks
    block = _block_size(chunk_waves)
    steps = chunk_waves // block
    first = chunk * steps
    ids = lax.dynamic_slice_in_dim(local_ids, chunk * chunk_waves, chunk_waves)
    return pl.pallas_call(
        legendre_kernel,
        out_shape=jax.ShapeDtypeStruct((1, bands, chunk_waves, rows, width), jnp.bfloat16),
        grid_spec=pltpu.PrefetchScalarGridSpec(
            num_scalar_prefetch=1,
            grid=(steps,),
            in_specs=[
                pl.BlockSpec((block, width, degree_count), lambda i, ids: (first + i, 0, 0)),
                pl.BlockSpec((block, lats, degree_count), lambda i, ids: (first + i, 0, 0)),
            ],
            out_specs=pl.BlockSpec((1, bands, block, rows, width), lambda i, ids: (0, 0, i, 0, 0)),
        ),
    )(ids, coef, leg)[0]


def per_device(spec_coef, legendre, wave_ids, dep_drow, dep_dlon, dep_frac):
    lat_count = lax.axis_size("lat")
    lon_parts = lax.axis_size("lon")
    local_waves = spec_coef.shape[0]
    level_fields = spec_coef.shape[2]
    degree_count = spec_coef.shape[3]
    all_waves = wave_ids.shape[0]
    row_count = dep_drow.shape[0]
    sector_width = dep_drow.shape[1]
    cycle_size = sector_width * lon_parts
    device = lax.axis_index("lat") * lon_parts + lax.axis_index("lon")
    local_ids = lax.dynamic_slice_in_dim(wave_ids, device * local_waves, local_waves)
    coef = spec_coef.reshape(local_waves, 2 * level_fields, degree_count)
    chunks = 2 if local_waves % 2 == 0 else 1
    chunk_waves = local_waves // chunks
    lon_start = lax.axis_index("lon") * sector_width
    by_chunk = wave_ids.reshape(lat_count, lon_parts, chunks, chunk_waves)
    margin = REACH + 1
    edge_cols = lon_start + jnp.concatenate(
        [jnp.arange(-margin, 0, dtype=jnp.int32), sector_width + jnp.arange(margin, dtype=jnp.int32)]
    )
    total = None
    for c in range(chunks):
        fourier = legendre_transform(local_ids, coef, legendre, lat_count, chunks, c)
        moved = lax.all_to_all(fourier, "lat", split_axis=0, concat_axis=0, tiled=True)
        gathered = lax.all_gather(moved, "lon", axis=0, tiled=True)
        gathered = gathered.reshape(lon_parts * lat_count * chunk_waves, row_count, 2, level_fields)
        wave_order = by_chunk[:, :, c, :].transpose(1, 0, 2).reshape(-1)
        table = wave_table(wave_order, lon_start, sector_width, cycle_size)
        side = edge_table(wave_order, edge_cols, cycle_size)
        table = jnp.concatenate([side[:, :, :margin], table, side[:, :, margin:]], axis=2)
        part = jnp.einsum("mprq,rmx->qpx", gathered, table, preferred_element_type=jnp.float32)
        total = part if total is None else total + part
    wide = total.astype(jnp.bfloat16)
    grid = wide[:, :, margin : margin + sector_width]
    padded = padded_2(wide, (("lat", 1),), margin, False)
    frac_row = dep_frac[0]
    frac_col = dep_frac[1]
    col_weights = [shift_weight(dep_dlon, frac_col, shift) for shift in range(-REACH, REACH + 2)]
    total = jnp.zeros((level_fields, row_count, sector_width), jnp.float32)
    for row_shift in range(-REACH, REACH + 2):
        band = padded[:, margin + row_shift : margin + row_shift + row_count, :]
        along = jnp.zeros((level_fields, row_count, sector_width), jnp.float32)
        for place, col_shift in enumerate(range(-REACH, REACH + 2)):
            window = band[:, :, margin + col_shift : margin + col_shift + sector_width].astype(
                jnp.float32
            )
            along = along + col_weights[place][None] * window
        total = total + shift_weight(dep_drow, frac_row, row_shift)[None] * along
    return (grid, total.astype(jnp.bfloat16))


def solution(mesh):
    in_specs = (
        P(("lat", "lon"), None, None, None),
        P(("lat", "lon"), None, None),
        P(),
        P("lat", "lon"),
        P("lat", "lon"),
        P(None, "lat", "lon"),
    )
    out_specs = (P(None, "lat", "lon"), P(None, "lat", "lon"))
    return jax.shard_map(
        per_device, mesh=mesh, in_specs=in_specs, out_specs=out_specs, check_vma=False
    )
```

```python
import math

import jax
import jax.numpy as jnp
from jax import lax
from jax.experimental import pallas as pl
from jax.experimental.pallas import tpu as pltpu
from jax.sharding import PartitionSpec as P

REACH = 1


def padded_2(cells, sides, width, closed):
    for axis, dim in sides:
        count = lax.axis_size(axis)
        ends = count if closed else count - 1
        head = lax.slice_in_dim(cells, 0, width, axis=dim)
        tail = lax.slice_in_dim(cells, cells.shape[dim] - width, cells.shape[dim], axis=dim)
        cells = jnp.concatenate(
            [
                lax.ppermute(tail, axis, [(i, (i + 1) % count) for i in range(ends)]),
                cells,
                lax.ppermute(head, axis, [((i + 1) % count, i) for i in range(ends)]),
            ],
            axis=dim,
        )
    return cells


def wave_table(wave_order, lon_start, lon_count, cycle_size):
    inner = 128 if lon_count % 128 == 0 else lon_count
    outer = lon_count // inner
    coarse = lon_start + inner * jnp.arange(outer, dtype=jnp.int32)
    fine = jnp.arange(inner, dtype=jnp.int32)
    scale = 2.0 * math.pi / cycle_size
    theta_a = (wave_order[:, None] * coarse[None, :] % cycle_size).astype(jnp.float32) * scale
    theta_b = (wave_order[:, None] * fine[None, :] % cycle_size).astype(jnp.float32) * scale
    cos_a = jnp.cos(theta_a)[:, :, None]
    sin_a = jnp.sin(theta_a)[:, :, None]
    cos_b = jnp.cos(theta_b)[:, None, :]
    sin_b = jnp.sin(theta_b)[:, None, :]
    factor = jnp.where(wave_order == 0, 1.0, 2.0).astype(jnp.float32)[:, None, None]
    real = factor * (cos_a * cos_b - sin_a * sin_b)
    imag = -factor * (sin_a * cos_b + cos_a * sin_b)
    count = wave_order.shape[0]
    return jnp.stack([real.reshape(count, lon_count), imag.reshape(count, lon_count)]).astype(
        jnp.bfloat16
    )


def edge_table(wave_order, columns, cycle_size):
    phase_index = wave_order[:, None] * (columns[None, :] % cycle_size) % cycle_size
    theta = phase_index.astype(jnp.float32) * (2.0 * math.pi / cycle_size)
    factor = jnp.where(wave_order == 0, 1.0, 2.0).astype(jnp.float32)[:, None]
    return jnp.stack([factor * jnp.cos(theta), -factor * jnp.sin(theta)]).astype(jnp.bfloat16)


def _block_size(count):
    for size in (8, 5, 4, 2, 1):
        if count % size == 0:
            return size
    return 1


def legendre_kernel(ids_ref, coef_ref, leg_ref, out_ref):
    step = pl.program_id(0)
    block = coef_ref.shape[0]
    bands = out_ref.shape[1]
    rows = out_ref.shape[3]
    degree_count = coef_ref.shape[2]
    degree = lax.broadcasted_iota(jnp.int32, (1, degree_count), 1)
    for w in range(block):
        wave = ids_ref[step * block + w]
        coef = coef_ref[w]
        kept = jnp.where(degree >= wave, coef, jnp.zeros((), coef.dtype))
        prod = lax.dot_general(
            leg_ref[w], kept, (((1,), (1,)), ((), ())), preferred_element_type=jnp.float32
        )
        out_ref[0, :, w, :, :] = prod.astype(out_ref.dtype).reshape(bands, rows, prod.shape[1])


def legendre_transform(local_ids, coef, leg, bands, chunks, chunk):
    local_waves, width, degree_count = coef.shape
    lats = leg.shape[1]
    rows = lats // bands
    chunk_waves = local_waves // chunks
    block = _block_size(chunk_waves)
    steps = chunk_waves // block
    first = chunk * steps
    ids = lax.dynamic_slice_in_dim(local_ids, chunk * chunk_waves, chunk_waves)
    return pl.pallas_call(
        legendre_kernel,
        out_shape=jax.ShapeDtypeStruct((1, bands, chunk_waves, rows, width), jnp.bfloat16),
        grid_spec=pltpu.PrefetchScalarGridSpec(
            num_scalar_prefetch=1,
            grid=(steps,),
            in_specs=[
                pl.BlockSpec((block, width, degree_count), lambda i, ids: (first + i, 0, 0)),
                pl.BlockSpec((block, lats, degree_count), lambda i, ids: (first + i, 0, 0)),
            ],
            out_specs=pl.BlockSpec((1, bands, block, rows, width), lambda i, ids: (0, 0, i, 0, 0)),
        ),
    )(ids, coef, leg)[0]


def per_device(spec_coef, legendre, wave_ids, dep_drow, dep_dlon, dep_frac):
    lat_count = lax.axis_size("lat")
    lon_parts = lax.axis_size("lon")
    local_waves = spec_coef.shape[0]
    level_fields = spec_coef.shape[2]
    degree_count = spec_coef.shape[3]
    all_waves = wave_ids.shape[0]
    row_count = dep_drow.shape[0]
    sector_width = dep_drow.shape[1]
    cycle_size = sector_width * lon_parts
    device = lax.axis_index("lat") * lon_parts + lax.axis_index("lon")
    local_ids = lax.dynamic_slice_in_dim(wave_ids, device * local_waves, local_waves)
    coef = spec_coef.reshape(local_waves, 2 * level_fields, degree_count)
    chunks = 2 if local_waves % 2 == 0 else 1
    chunk_waves = local_waves // chunks
    lon_start = lax.axis_index("lon") * sector_width
    by_chunk = wave_ids.reshape(lat_count, lon_parts, chunks, chunk_waves)
    margin = REACH + 1
    edge_cols = lon_start + jnp.concatenate(
        [jnp.arange(-margin, 0, dtype=jnp.int32), sector_width + jnp.arange(margin, dtype=jnp.int32)]
    )
    total = None
    for c in range(chunks):
        fourier = legendre_transform(local_ids, coef, legendre, lat_count, chunks, c)
        moved = lax.all_to_all(fourier, "lat", split_axis=0, concat_axis=0, tiled=True)
        gathered = lax.all_gather(moved, "lon", axis=0, tiled=True)
        gathered = gathered.reshape(lon_parts * lat_count * chunk_waves, row_count, 2, level_fields)
        wave_order = by_chunk[:, :, c, :].transpose(1, 0, 2).reshape(-1)
        table = wave_table(wave_order, lon_start, sector_width, cycle_size)
        side = edge_table(wave_order, edge_cols, cycle_size)
        table = jnp.concatenate([side[:, :, :margin], table, side[:, :, margin:]], axis=2)
        part = jnp.einsum("mprq,rmx->qpx", gathered, table, preferred_element_type=jnp.float32)
        total = part if total is None else total + part
    wide = total.astype(jnp.bfloat16)
    grid = wide[:, :, margin : margin + sector_width]
    padded = padded_2(wide, (("lat", 1),), margin, False)
    frac_row = dep_frac[0][None]
    frac_col = dep_frac[1][None]
    col_at = [(dep_dlon == v)[None] for v in range(-REACH, REACH)]
    row_at = [(dep_drow == v)[None] for v in range(-REACH, REACH)]

    def pick(masks, values, extra):
        out = values[2 * REACH + extra]
        for place, mask in enumerate(masks):
            out = jnp.where(mask, values[place + extra], out)
        return out

    along = []
    for row_shift in range(-REACH, REACH + 2):
        band = padded[:, margin + row_shift : margin + row_shift + row_count, :]
        windows = [
            band[:, :, margin + col_shift : margin + col_shift + sector_width]
            for col_shift in range(-REACH, REACH + 2)
        ]
        lower = pick(col_at, windows, 0).astype(jnp.float32)
        upper = pick(col_at, windows, 1).astype(jnp.float32)
        along.append(lower + frac_col * (upper - lower))
    lower = pick(row_at, along, 0)
    upper = pick(row_at, along, 1)
    total = lower + frac_row * (upper - lower)
    return (grid, total.astype(jnp.bfloat16))


def solution(mesh):
    in_specs = (
        P(("lat", "lon"), None, None, None),
        P(("lat", "lon"), None, None),
        P(),
        P("lat", "lon"),
        P("lat", "lon"),
        P(None, "lat", "lon"),
    )
    out_specs = (P(None, "lat", "lon"), P(None, "lat", "lon"))
    return jax.shard_map(
        per_device, mesh=mesh, in_specs=in_specs, out_specs=out_specs, check_vma=False
    )
```

```python
import math

import jax
import jax.numpy as jnp
from jax import lax
from jax.experimental import pallas as pl
from jax.experimental.pallas import tpu as pltpu
from jax.sharding import PartitionSpec as P

REACH = 1


def padded_2(cells, sides, width, closed):
    for axis, dim in sides:
        count = lax.axis_size(axis)
        ends = count if closed else count - 1
        head = lax.slice_in_dim(cells, 0, width, axis=dim)
        tail = lax.slice_in_dim(cells, cells.shape[dim] - width, cells.shape[dim], axis=dim)
        cells = jnp.concatenate(
            [
                lax.ppermute(tail, axis, [(i, (i + 1) % count) for i in range(ends)]),
                cells,
                lax.ppermute(head, axis, [((i + 1) % count, i) for i in range(ends)]),
            ],
            axis=dim,
        )
    return cells


def wave_table(wave_order, lon_start, lon_count, cycle_size):
    inner = 128 if lon_count % 128 == 0 else lon_count
    outer = lon_count // inner
    coarse = lon_start + inner * jnp.arange(outer, dtype=jnp.int32)
    fine = jnp.arange(inner, dtype=jnp.int32)
    scale = 2.0 * math.pi / cycle_size
    theta_a = (wave_order[:, None] * coarse[None, :] % cycle_size).astype(jnp.float32) * scale
    theta_b = (wave_order[:, None] * fine[None, :] % cycle_size).astype(jnp.float32) * scale
    cos_a = jnp.cos(theta_a)[:, :, None]
    sin_a = jnp.sin(theta_a)[:, :, None]
    cos_b = jnp.cos(theta_b)[:, None, :]
    sin_b = jnp.sin(theta_b)[:, None, :]
    factor = jnp.where(wave_order == 0, 1.0, 2.0).astype(jnp.float32)[:, None, None]
    real = factor * (cos_a * cos_b - sin_a * sin_b)
    imag = -factor * (sin_a * cos_b + cos_a * sin_b)
    count = wave_order.shape[0]
    return jnp.stack([real.reshape(count, lon_count), imag.reshape(count, lon_count)]).astype(
        jnp.bfloat16
    )


def edge_table(wave_order, columns, cycle_size):
    phase_index = wave_order[:, None] * (columns[None, :] % cycle_size) % cycle_size
    theta = phase_index.astype(jnp.float32) * (2.0 * math.pi / cycle_size)
    factor = jnp.where(wave_order == 0, 1.0, 2.0).astype(jnp.float32)[:, None]
    return jnp.stack([factor * jnp.cos(theta), -factor * jnp.sin(theta)]).astype(jnp.bfloat16)


def shift_weight(offsets, frac, shift):
    zeros = jnp.zeros_like(frac)
    lower = jnp.where(offsets == shift, 1.0 - frac, zeros)
    higher = jnp.where(offsets == shift - 1, frac, zeros)
    return lower + higher


def _block_size(count):
    for size in (8, 5, 4, 2, 1):
        if count % size == 0:
            return size
    return 1


def legendre_kernel(ids_ref, coef_ref, leg_ref, out_ref):
    step = pl.program_id(0)
    block = coef_ref.shape[0]
    bands = out_ref.shape[1]
    rows = out_ref.shape[3]
    degree_count = coef_ref.shape[2]
    degree = lax.broadcasted_iota(jnp.int32, (1, degree_count), 1)
    for w in range(block):
        wave = ids_ref[step * block + w]
        coef = coef_ref[w]
        kept = jnp.where(degree >= wave, coef, jnp.zeros((), coef.dtype))
        prod = lax.dot_general(
            leg_ref[w], kept, (((1,), (1,)), ((), ())), preferred_element_type=jnp.float32
        )
        out_ref[0, :, w, :, :] = prod.astype(out_ref.dtype).reshape(bands, rows, prod.shape[1])


def legendre_transform(local_ids, coef, leg, bands, chunks, chunk):
    local_waves, width, degree_count = coef.shape
    lats = leg.shape[1]
    rows = lats // bands
    chunk_waves = local_waves // chunks
    block = _block_size(chunk_waves)
    steps = chunk_waves // block
    first = chunk * steps
    ids = lax.dynamic_slice_in_dim(local_ids, chunk * chunk_waves, chunk_waves)
    return pl.pallas_call(
        legendre_kernel,
        out_shape=jax.ShapeDtypeStruct((1, bands, chunk_waves, rows, width), jnp.bfloat16),
        grid_spec=pltpu.PrefetchScalarGridSpec(
            num_scalar_prefetch=1,
            grid=(steps,),
            in_specs=[
                pl.BlockSpec((block, width, degree_count), lambda i, ids: (first + i, 0, 0)),
                pl.BlockSpec((block, lats, degree_count), lambda i, ids: (first + i, 0, 0)),
            ],
            out_specs=pl.BlockSpec((1, bands, block, rows, width), lambda i, ids: (0, 0, i, 0, 0)),
        ),
    )(ids, coef, leg)[0]


def per_device(spec_coef, legendre, wave_ids, dep_drow, dep_dlon, dep_frac):
    lat_count = lax.axis_size("lat")
    lon_parts = lax.axis_size("lon")
    local_waves = spec_coef.shape[0]
    level_fields = spec_coef.shape[2]
    degree_count = spec_coef.shape[3]
    all_waves = wave_ids.shape[0]
    row_count = dep_drow.shape[0]
    sector_width = dep_drow.shape[1]
    cycle_size = sector_width * lon_parts
    device = lax.axis_index("lat") * lon_parts + lax.axis_index("lon")
    local_ids = lax.dynamic_slice_in_dim(wave_ids, device * local_waves, local_waves)
    coef = spec_coef.reshape(local_waves, 2 * level_fields, degree_count)
    chunks = 2 if local_waves % 2 == 0 else 1
    chunk_waves = local_waves // chunks
    lon_start = lax.axis_index("lon") * sector_width
    by_chunk = wave_ids.reshape(lat_count, lon_parts, chunks, chunk_waves)
    margin = REACH + 1
    edge_cols = lon_start + jnp.concatenate(
        [jnp.arange(-margin, 0, dtype=jnp.int32), sector_width + jnp.arange(margin, dtype=jnp.int32)]
    )
    total = None
    for c in range(chunks):
        fourier = legendre_transform(local_ids, coef, legendre, lat_count, chunks, c)
        moved = lax.all_to_all(fourier, "lat", split_axis=0, concat_axis=0, tiled=True)
        gathered = lax.all_gather(moved, "lon", axis=0, tiled=True)
        gathered = gathered.reshape(lon_parts * lat_count * chunk_waves, row_count, 2, level_fields)
        wave_order = by_chunk[:, :, c, :].transpose(1, 0, 2).reshape(-1)
        table = wave_table(wave_order, lon_start, sector_width, cycle_size)
        side = edge_table(wave_order, edge_cols, cycle_size)
        table = jnp.concatenate([side[:, :, :margin], table, side[:, :, margin:]], axis=2)
        part = jnp.einsum("mprq,rmx->qpx", gathered, table, preferred_element_type=jnp.float32)
        total = part if total is None else total + part
    wide = total.astype(jnp.bfloat16)
    grid = wide[:, :, margin : margin + sector_width]
    padded = padded_2(wide, (("lat", 1),), margin, False)
    padded = lax.optimization_barrier(padded)
    frac_row = dep_frac[0]
    frac_col = dep_frac[1]
    shifts = range(-REACH, REACH + 2)
    col_weights = [shift_weight(dep_dlon, frac_col, shift) for shift in shifts]
    row_weights = [shift_weight(dep_drow, frac_row, shift) for shift in shifts]
    weights = jnp.stack([r * c for r in row_weights for c in col_weights])
    total = jnp.zeros((level_fields, row_count, sector_width), jnp.float32)
    place = 0
    for row_shift in shifts:
        band = padded[:, margin + row_shift : margin + row_shift + row_count, :]
        for col_shift in shifts:
            window = band[:, :, margin + col_shift : margin + col_shift + sector_width]
            total = total + weights[place][None] * window.astype(jnp.float32)
            place += 1
    return (grid, total.astype(jnp.bfloat16))


def solution(mesh):
    in_specs = (
        P(("lat", "lon"), None, None, None),
        P(("lat", "lon"), None, None),
        P(),
        P("lat", "lon"),
        P("lat", "lon"),
        P(None, "lat", "lon"),
    )
    out_specs = (P(None, "lat", "lon"), P(None, "lat", "lon"))
    return jax.shard_map(
        per_device, mesh=mesh, in_specs=in_specs, out_specs=out_specs, check_vma=False
    )
```

```python
import math

import jax
import jax.numpy as jnp
from jax import lax
from jax.experimental import pallas as pl
from jax.experimental.pallas import tpu as pltpu
from jax.sharding import PartitionSpec as P

REACH = 1


def padded_2(cells, sides, width, closed):
    for axis, dim in sides:
        count = lax.axis_size(axis)
        ends = count if closed else count - 1
        head = lax.slice_in_dim(cells, 0, width, axis=dim)
        tail = lax.slice_in_dim(cells, cells.shape[dim] - width, cells.shape[dim], axis=dim)
        cells = jnp.concatenate(
            [
                lax.ppermute(tail, axis, [(i, (i + 1) % count) for i in range(ends)]),
                cells,
                lax.ppermute(head, axis, [((i + 1) % count, i) for i in range(ends)]),
            ],
            axis=dim,
        )
    return cells


def wave_table(wave_order, lon_start, lon_count, cycle_size):
    inner = 128
    outer = -(-lon_count // inner)
    coarse = lon_start + inner * jnp.arange(outer, dtype=jnp.int32)
    fine = jnp.arange(inner, dtype=jnp.int32)
    scale = 2.0 * math.pi / cycle_size
    theta_a = (wave_order[:, None] * coarse[None, :] % cycle_size).astype(jnp.float32) * scale
    theta_b = (wave_order[:, None] * fine[None, :] % cycle_size).astype(jnp.float32) * scale
    cos_a = jnp.cos(theta_a)[:, :, None]
    sin_a = jnp.sin(theta_a)[:, :, None]
    cos_b = jnp.cos(theta_b)[:, None, :]
    sin_b = jnp.sin(theta_b)[:, None, :]
    factor = jnp.where(wave_order == 0, 1.0, 2.0).astype(jnp.float32)[:, None, None]
    real = factor * (cos_a * cos_b - sin_a * sin_b)
    imag = -factor * (sin_a * cos_b + cos_a * sin_b)
    count = wave_order.shape[0]
    width = outer * inner
    return jnp.stack(
        [real.reshape(count, width)[:, :lon_count], imag.reshape(count, width)[:, :lon_count]]
    ).astype(jnp.bfloat16)


def shift_weight(offsets, frac, shift):
    zeros = jnp.zeros_like(frac)
    lower = jnp.where(offsets == shift, 1.0 - frac, zeros)
    higher = jnp.where(offsets == shift - 1, frac, zeros)
    return lower + higher


def _block_size(count):
    for size in (8, 5, 4, 2, 1):
        if count % size == 0:
            return size
    return 1


def legendre_kernel(ids_ref, coef_ref, leg_ref, out_ref):
    step = pl.program_id(0)
    block = coef_ref.shape[0]
    bands = out_ref.shape[1]
    rows = out_ref.shape[3]
    degree_count = coef_ref.shape[2]
    degree = lax.broadcasted_iota(jnp.int32, (1, degree_count), 1)
    for w in range(block):
        wave = ids_ref[step * block + w]
        coef = coef_ref[w]
        kept = jnp.where(degree >= wave, coef, jnp.zeros((), coef.dtype))
        prod = lax.dot_general(
            leg_ref[w], kept, (((1,), (1,)), ((), ())), preferred_element_type=jnp.float32
        )
        out_ref[0, :, w, :, :] = prod.astype(out_ref.dtype).reshape(bands, rows, prod.shape[1])


def legendre_transform(local_ids, coef, leg, bands, chunks, chunk):
    local_waves, width, degree_count = coef.shape
    lats = leg.shape[1]
    rows = lats // bands
    chunk_waves = local_waves // chunks
    block = _block_size(chunk_waves)
    steps = chunk_waves // block
    first = chunk * steps
    ids = lax.dynamic_slice_in_dim(local_ids, chunk * chunk_waves, chunk_waves)
    return pl.pallas_call(
        legendre_kernel,
        out_shape=jax.ShapeDtypeStruct((1, bands, chunk_waves, rows, width), jnp.bfloat16),
        grid_spec=pltpu.PrefetchScalarGridSpec(
            num_scalar_prefetch=1,
            grid=(steps,),
            in_specs=[
                pl.BlockSpec((block, width, degree_count), lambda i, ids: (first + i, 0, 0)),
                pl.BlockSpec((block, lats, degree_count), lambda i, ids: (first + i, 0, 0)),
            ],
            out_specs=pl.BlockSpec((1, bands, block, rows, width), lambda i, ids: (0, 0, i, 0, 0)),
        ),
    )(ids, coef, leg)[0]


def per_device(spec_coef, legendre, wave_ids, dep_drow, dep_dlon, dep_frac):
    lat_count = lax.axis_size("lat")
    lon_parts = lax.axis_size("lon")
    local_waves = spec_coef.shape[0]
    level_fields = spec_coef.shape[2]
    degree_count = spec_coef.shape[3]
    all_waves = wave_ids.shape[0]
    row_count = dep_drow.shape[0]
    sector_width = dep_drow.shape[1]
    cycle_size = sector_width * lon_parts
    device = lax.axis_index("lat") * lon_parts + lax.axis_index("lon")
    local_ids = lax.dynamic_slice_in_dim(wave_ids, device * local_waves, local_waves)
    coef = spec_coef.reshape(local_waves, 2 * level_fields, degree_count)
    chunks = 2 if local_waves % 2 == 0 else 1
    chunk_waves = local_waves // chunks
    lon_start = lax.axis_index("lon") * sector_width
    by_chunk = wave_ids.reshape(lat_count, lon_parts, chunks, chunk_waves)
    margin = REACH + 1
    total = None
    for c in range(chunks):
        fourier = legendre_transform(local_ids, coef, legendre, lat_count, chunks, c)
        moved = lax.all_to_all(fourier, "lat", split_axis=0, concat_axis=0, tiled=True)
        gathered = lax.all_gather(moved, "lon", axis=0, tiled=True)
        gathered = gathered.reshape(lon_parts * lat_count * chunk_waves, row_count, 2, level_fields)
        wave_order = by_chunk[:, :, c, :].transpose(1, 0, 2).reshape(-1)
        table = wave_table(wave_order, lon_start - margin, sector_width + 2 * margin, cycle_size)
        part = jnp.einsum("mprq,rmx->qpx", gathered, table, preferred_element_type=jnp.float32)
        total = part if total is None else total + part
    wide = total.astype(jnp.bfloat16)
    grid = wide[:, :, margin : margin + sector_width]
    padded = padded_2(wide, (("lat", 1),), margin, False)
    padded = lax.optimization_barrier(padded)
    frac_row = dep_frac[0]
    frac_col = dep_frac[1]
    shifts = range(-REACH, REACH + 2)
    col_weights = [shift_weight(dep_dlon, frac_col, shift) for shift in shifts]
    row_weights = [shift_weight(dep_drow, frac_row, shift) for shift in shifts]
    weights = jnp.stack([r * c for r in row_weights for c in col_weights])
    total = jnp.zeros((level_fields, row_count, sector_width), jnp.float32)
    place = 0
    for row_shift in shifts:
        band = padded[:, margin + row_shift : margin + row_shift + row_count, :]
        for col_shift in shifts:
            window = band[:, :, margin + col_shift : margin + col_shift + sector_width]
            total = total + weights[place][None] * window.astype(jnp.float32)
            place += 1
    return (grid, total.astype(jnp.bfloat16))


def solution(mesh):
    in_specs = (
        P(("lat", "lon"), None, None, None),
        P(("lat", "lon"), None, None),
        P(),
        P("lat", "lon"),
        P("lat", "lon"),
        P(None, "lat", "lon"),
    )
    out_specs = (P(None, "lat", "lon"), P(None, "lat", "lon"))
    return jax.shard_map(
        per_device, mesh=mesh, in_specs=in_specs, out_specs=out_specs, check_vma=False
    )
```

```python
import math

import jax
import jax.numpy as jnp
from jax import lax
from jax.experimental import pallas as pl
from jax.experimental.layout import Layout, with_layout_constraint
from jax.experimental.pallas import tpu as pltpu
from jax.sharding import PartitionSpec as P

REACH = 1


def padded_2(cells, sides, width, closed):
    for axis, dim in sides:
        count = lax.axis_size(axis)
        ends = count if closed else count - 1
        head = lax.slice_in_dim(cells, 0, width, axis=dim)
        tail = lax.slice_in_dim(cells, cells.shape[dim] - width, cells.shape[dim], axis=dim)
        cells = jnp.concatenate(
            [
                lax.ppermute(tail, axis, [(i, (i + 1) % count) for i in range(ends)]),
                cells,
                lax.ppermute(head, axis, [((i + 1) % count, i) for i in range(ends)]),
            ],
            axis=dim,
        )
    return cells


def wave_table(wave_order, lon_start, lon_count, cycle_size):
    inner = 128
    outer = -(-lon_count // inner)
    coarse = lon_start + inner * jnp.arange(outer, dtype=jnp.int32)
    fine = jnp.arange(inner, dtype=jnp.int32)
    scale = 2.0 * math.pi / cycle_size
    theta_a = (wave_order[:, None] * coarse[None, :] % cycle_size).astype(jnp.float32) * scale
    theta_b = (wave_order[:, None] * fine[None, :] % cycle_size).astype(jnp.float32) * scale
    cos_a = jnp.cos(theta_a)[:, :, None]
    sin_a = jnp.sin(theta_a)[:, :, None]
    cos_b = jnp.cos(theta_b)[:, None, :]
    sin_b = jnp.sin(theta_b)[:, None, :]
    factor = jnp.where(wave_order == 0, 1.0, 2.0).astype(jnp.float32)[:, None, None]
    real = factor * (cos_a * cos_b - sin_a * sin_b)
    imag = -factor * (sin_a * cos_b + cos_a * sin_b)
    count = wave_order.shape[0]
    width = outer * inner
    return jnp.stack(
        [real.reshape(count, width)[:, :lon_count], imag.reshape(count, width)[:, :lon_count]]
    ).astype(jnp.bfloat16)


def shift_weight(offsets, frac, shift):
    zeros = jnp.zeros_like(frac)
    lower = jnp.where(offsets == shift, 1.0 - frac, zeros)
    higher = jnp.where(offsets == shift - 1, frac, zeros)
    return lower + higher


def _block_size(count):
    for size in (8, 5, 4, 2, 1):
        if count % size == 0:
            return size
    return 1


def legendre_kernel(ids_ref, coef_ref, leg_ref, out_ref):
    step = pl.program_id(0)
    block = coef_ref.shape[0]
    bands = out_ref.shape[1]
    rows = out_ref.shape[3]
    degree_count = coef_ref.shape[2]
    degree = lax.broadcasted_iota(jnp.int32, (1, degree_count), 1)
    for w in range(block):
        wave = ids_ref[step * block + w]
        coef = coef_ref[w]
        kept = jnp.where(degree >= wave, coef, jnp.zeros((), coef.dtype))
        prod = lax.dot_general(
            leg_ref[w], kept, (((1,), (1,)), ((), ())), preferred_element_type=jnp.float32
        )
        out_ref[0, :, w, :, :] = prod.astype(out_ref.dtype).reshape(bands, rows, prod.shape[1])


def legendre_transform(local_ids, coef, leg, bands, chunks, chunk):
    local_waves, width, degree_count = coef.shape
    lats = leg.shape[1]
    rows = lats // bands
    chunk_waves = local_waves // chunks
    block = _block_size(chunk_waves)
    steps = chunk_waves // block
    first = chunk * steps
    ids = lax.dynamic_slice_in_dim(local_ids, chunk * chunk_waves, chunk_waves)
    return pl.pallas_call(
        legendre_kernel,
        out_shape=jax.ShapeDtypeStruct((1, bands, chunk_waves, rows, width), jnp.bfloat16),
        grid_spec=pltpu.PrefetchScalarGridSpec(
            num_scalar_prefetch=1,
            grid=(steps,),
            in_specs=[
                pl.BlockSpec((block, width, degree_count), lambda i, ids: (first + i, 0, 0)),
                pl.BlockSpec((block, lats, degree_count), lambda i, ids: (first + i, 0, 0)),
            ],
            out_specs=pl.BlockSpec((1, bands, block, rows, width), lambda i, ids: (0, 0, i, 0, 0)),
        ),
    )(ids, coef, leg)[0]


def per_device(spec_coef, legendre, wave_ids, dep_drow, dep_dlon, dep_frac):
    lat_count = lax.axis_size("lat")
    lon_parts = lax.axis_size("lon")
    local_waves = spec_coef.shape[0]
    level_fields = spec_coef.shape[2]
    degree_count = spec_coef.shape[3]
    all_waves = wave_ids.shape[0]
    row_count = dep_drow.shape[0]
    sector_width = dep_drow.shape[1]
    cycle_size = sector_width * lon_parts
    device = lax.axis_index("lat") * lon_parts + lax.axis_index("lon")
    local_ids = lax.dynamic_slice_in_dim(wave_ids, device * local_waves, local_waves)
    coef = spec_coef.reshape(local_waves, 2 * level_fields, degree_count)
    chunks = 2 if local_waves % 2 == 0 else 1
    chunk_waves = local_waves // chunks
    lon_start = lax.axis_index("lon") * sector_width
    by_chunk = wave_ids.reshape(lat_count, lon_parts, chunks, chunk_waves)
    margin = REACH + 1
    total = None
    for c in range(chunks):
        fourier = legendre_transform(local_ids, coef, legendre, lat_count, chunks, c)
        moved = lax.all_to_all(fourier, "lat", split_axis=0, concat_axis=0, tiled=True)
        gathered = lax.all_gather(moved, "lon", axis=0, tiled=True)
        gathered = gathered.reshape(lon_parts * lat_count * chunk_waves, row_count, 2, level_fields)
        wave_order = by_chunk[:, :, c, :].transpose(1, 0, 2).reshape(-1)
        table = wave_table(wave_order, lon_start - margin, sector_width + 2 * margin, cycle_size)
        part = jnp.einsum("mprq,rmx->qpx", gathered, table, preferred_element_type=jnp.float32)
        total = part if total is None else total + part
    wide = total.astype(jnp.bfloat16)
    grid = wide[:, :, margin : margin + sector_width]
    padded = padded_2(wide, (("lat", 1),), margin, False)
    padded = lax.optimization_barrier(padded)
    frac_row = dep_frac[0]
    frac_col = dep_frac[1]
    shifts = range(-REACH, REACH + 2)
    col_weights = [shift_weight(dep_dlon, frac_col, shift) for shift in shifts]
    row_weights = [shift_weight(dep_drow, frac_row, shift) for shift in shifts]
    weights = jnp.stack([r * c for r in row_weights for c in col_weights])
    total = jnp.zeros((level_fields, row_count, sector_width), jnp.float32)
    place = 0
    for row_shift in shifts:
        band = padded[:, margin + row_shift : margin + row_shift + row_count, :]
        for col_shift in shifts:
            window = band[:, :, margin + col_shift : margin + col_shift + sector_width]
            total = total + weights[place][None] * window.astype(jnp.float32)
            place += 1
    departed = with_layout_constraint(total.astype(jnp.bfloat16), Layout((0, 1, 2)))
    return (grid, departed)


def solution(mesh):
    in_specs = (
        P(("lat", "lon"), None, None, None),
        P(("lat", "lon"), None, None),
        P(),
        P("lat", "lon"),
        P("lat", "lon"),
        P(None, "lat", "lon"),
    )
    out_specs = (P(None, "lat", "lon"), P(None, "lat", "lon"))
    return jax.shard_map(
        per_device, mesh=mesh, in_specs=in_specs, out_specs=out_specs, check_vma=False
    )
```

```python
import math

import jax
import jax.numpy as jnp
from jax import lax
from jax.experimental import pallas as pl
from jax.experimental.pallas import tpu as pltpu
from jax.sharding import PartitionSpec as P

REACH = 1


def padded_2(cells, sides, width, closed):
    for axis, dim in sides:
        count = lax.axis_size(axis)
        ends = count if closed else count - 1
        head = lax.slice_in_dim(cells, 0, width, axis=dim)
        tail = lax.slice_in_dim(cells, cells.shape[dim] - width, cells.shape[dim], axis=dim)
        cells = jnp.concatenate(
            [
                lax.ppermute(tail, axis, [(i, (i + 1) % count) for i in range(ends)]),
                cells,
                lax.ppermute(head, axis, [((i + 1) % count, i) for i in range(ends)]),
            ],
            axis=dim,
        )
    return cells


def wave_table(wave_order, lon_start, lon_count, cycle_size):
    inner = 128
    outer = -(-lon_count // inner)
    coarse = lon_start + inner * jnp.arange(outer, dtype=jnp.int32)
    fine = jnp.arange(inner, dtype=jnp.int32)
    scale = 2.0 * math.pi / cycle_size
    theta_a = (wave_order[:, None] * coarse[None, :] % cycle_size).astype(jnp.float32) * scale
    theta_b = (wave_order[:, None] * fine[None, :] % cycle_size).astype(jnp.float32) * scale
    cos_a = jnp.cos(theta_a)[:, :, None]
    sin_a = jnp.sin(theta_a)[:, :, None]
    cos_b = jnp.cos(theta_b)[:, None, :]
    sin_b = jnp.sin(theta_b)[:, None, :]
    factor = jnp.where(wave_order == 0, 1.0, 2.0).astype(jnp.float32)[:, None, None]
    real = factor * (cos_a * cos_b - sin_a * sin_b)
    imag = -factor * (sin_a * cos_b + cos_a * sin_b)
    count = wave_order.shape[0]
    width = outer * inner
    return jnp.stack(
        [real.reshape(count, width)[:, :lon_count], imag.reshape(count, width)[:, :lon_count]]
    ).astype(jnp.bfloat16)


def shift_weight(offsets, frac, shift):
    zeros = jnp.zeros_like(frac)
    lower = jnp.where(offsets == shift, 1.0 - frac, zeros)
    higher = jnp.where(offsets == shift - 1, frac, zeros)
    return lower + higher


def _block_size(count):
    for size in (10, 8, 5, 4, 2, 1):
        if count % size == 0:
            return size
    return 1


def legendre_kernel(ids_ref, coef_ref, leg_ref, out_ref):
    step = pl.program_id(0)
    block = coef_ref.shape[0]
    bands = out_ref.shape[1]
    rows = out_ref.shape[3]
    degree_count = coef_ref.shape[2]
    degree = lax.broadcasted_iota(jnp.int32, (1, degree_count), 1)
    for w in range(block):
        wave = ids_ref[step * block + w]
        coef = coef_ref[w]
        kept = jnp.where(degree >= wave, coef, jnp.zeros((), coef.dtype))
        prod = lax.dot_general(
            leg_ref[w], kept, (((1,), (1,)), ((), ())), preferred_element_type=jnp.float32
        )
        out_ref[0, :, w, :, :] = prod.astype(out_ref.dtype).reshape(bands, rows, prod.shape[1])


def legendre_transform(local_ids, coef, leg, bands, chunks, chunk):
    local_waves, width, degree_count = coef.shape
    lats = leg.shape[1]
    rows = lats // bands
    chunk_waves = local_waves // chunks
    block = _block_size(chunk_waves)
    steps = chunk_waves // block
    first = chunk * steps
    ids = lax.dynamic_slice_in_dim(local_ids, chunk * chunk_waves, chunk_waves)
    return pl.pallas_call(
        legendre_kernel,
        out_shape=jax.ShapeDtypeStruct((1, bands, chunk_waves, rows, width), jnp.bfloat16),
        grid_spec=pltpu.PrefetchScalarGridSpec(
            num_scalar_prefetch=1,
            grid=(steps,),
            in_specs=[
                pl.BlockSpec((block, width, degree_count), lambda i, ids: (first + i, 0, 0)),
                pl.BlockSpec((block, lats, degree_count), lambda i, ids: (first + i, 0, 0)),
            ],
            out_specs=pl.BlockSpec((1, bands, block, rows, width), lambda i, ids: (0, 0, i, 0, 0)),
        ),
    )(ids, coef, leg)[0]


def per_device(spec_coef, legendre, wave_ids, dep_drow, dep_dlon, dep_frac):
    lat_count = lax.axis_size("lat")
    lon_parts = lax.axis_size("lon")
    local_waves = spec_coef.shape[0]
    level_fields = spec_coef.shape[2]
    degree_count = spec_coef.shape[3]
    all_waves = wave_ids.shape[0]
    row_count = dep_drow.shape[0]
    sector_width = dep_drow.shape[1]
    cycle_size = sector_width * lon_parts
    device = lax.axis_index("lat") * lon_parts + lax.axis_index("lon")
    local_ids = lax.dynamic_slice_in_dim(wave_ids, device * local_waves, local_waves)
    coef = spec_coef.reshape(local_waves, 2 * level_fields, degree_count)
    chunks = 2 if local_waves % 2 == 0 else 1
    chunk_waves = local_waves // chunks
    lon_start = lax.axis_index("lon") * sector_width
    by_chunk = wave_ids.reshape(lat_count, lon_parts, chunks, chunk_waves)
    margin = REACH + 1
    total = None
    for c in range(chunks):
        fourier = legendre_transform(local_ids, coef, legendre, lat_count, chunks, c)
        moved = lax.all_to_all(fourier, "lat", split_axis=0, concat_axis=0, tiled=True)
        gathered = lax.all_gather(moved, "lon", axis=0, tiled=True)
        gathered = gathered.reshape(lon_parts * lat_count * chunk_waves, row_count, 2, level_fields)
        wave_order = by_chunk[:, :, c, :].transpose(1, 0, 2).reshape(-1)
        table = wave_table(wave_order, lon_start - margin, sector_width + 2 * margin, cycle_size)
        part = jnp.einsum("mprq,rmx->qpx", gathered, table, preferred_element_type=jnp.float32)
        total = part if total is None else total + part
    wide = total.astype(jnp.bfloat16)
    grid = wide[:, :, margin : margin + sector_width]
    padded = padded_2(wide, (("lat", 1),), margin, False)
    padded = lax.optimization_barrier(padded)
    frac_row = dep_frac[0]
    frac_col = dep_frac[1]
    shifts = range(-REACH, REACH + 2)
    col_weights = [shift_weight(dep_dlon, frac_col, shift) for shift in shifts]
    row_weights = [shift_weight(dep_drow, frac_row, shift) for shift in shifts]
    weights = jnp.stack([r * c for r in row_weights for c in col_weights])
    total = jnp.zeros((level_fields, row_count, sector_width), jnp.float32)
    place = 0
    for row_shift in shifts:
        band = padded[:, margin + row_shift : margin + row_shift + row_count, :]
        for col_shift in shifts:
            window = band[:, :, margin + col_shift : margin + col_shift + sector_width]
            total = total + weights[place][None] * window.astype(jnp.float32)
            place += 1
    return (grid, total.astype(jnp.bfloat16))


def solution(mesh):
    in_specs = (
        P(("lat", "lon"), None, None, None),
        P(("lat", "lon"), None, None),
        P(),
        P("lat", "lon"),
        P("lat", "lon"),
        P(None, "lat", "lon"),
    )
    out_specs = (P(None, "lat", "lon"), P(None, "lat", "lon"))
    return jax.shard_map(
        per_device, mesh=mesh, in_specs=in_specs, out_specs=out_specs, check_vma=False
    )
```

```python
import math

import jax
import jax.numpy as jnp
from jax import lax
from jax.experimental import pallas as pl
from jax.experimental.pallas import tpu as pltpu
from jax.sharding import PartitionSpec as P

REACH = 1


def padded_2(cells, sides, width, closed):
    for axis, dim in sides:
        count = lax.axis_size(axis)
        ends = count if closed else count - 1
        head = lax.slice_in_dim(cells, 0, width, axis=dim)
        tail = lax.slice_in_dim(cells, cells.shape[dim] - width, cells.shape[dim], axis=dim)
        cells = jnp.concatenate(
            [
                lax.ppermute(tail, axis, [(i, (i + 1) % count) for i in range(ends)]),
                cells,
                lax.ppermute(head, axis, [((i + 1) % count, i) for i in range(ends)]),
            ],
            axis=dim,
        )
    return cells


def wave_table(wave_order, lon_start, lon_count, cycle_size):
    inner = 128
    outer = -(-lon_count // inner)
    coarse = lon_start + inner * jnp.arange(outer, dtype=jnp.int32)
    fine = jnp.arange(inner, dtype=jnp.int32)
    scale = 2.0 * math.pi / cycle_size
    theta_a = (wave_order[:, None] * coarse[None, :] % cycle_size).astype(jnp.float32) * scale
    theta_b = (wave_order[:, None] * fine[None, :] % cycle_size).astype(jnp.float32) * scale
    cos_a = jnp.cos(theta_a)[:, :, None]
    sin_a = jnp.sin(theta_a)[:, :, None]
    cos_b = jnp.cos(theta_b)[:, None, :]
    sin_b = jnp.sin(theta_b)[:, None, :]
    factor = jnp.where(wave_order == 0, 1.0, 2.0).astype(jnp.float32)[:, None, None]
    real = factor * (cos_a * cos_b - sin_a * sin_b)
    imag = -factor * (sin_a * cos_b + cos_a * sin_b)
    count = wave_order.shape[0]
    width = outer * inner
    return jnp.stack(
        [real.reshape(count, width)[:, :lon_count], imag.reshape(count, width)[:, :lon_count]]
    ).astype(jnp.bfloat16)


def shift_weight(offsets, frac, shift):
    zeros = jnp.zeros_like(frac)
    lower = jnp.where(offsets == shift, 1.0 - frac, zeros)
    higher = jnp.where(offsets == shift - 1, frac, zeros)
    return lower + higher


def _block_size(count):
    for size in (10, 8, 5, 4, 2, 1):
        if count % size == 0:
            return size
    return 1


def legendre_kernel(ids_ref, coef_ref, leg_ref, out_ref):
    step = pl.program_id(0)
    block = coef_ref.shape[0]
    bands = out_ref.shape[1]
    rows = out_ref.shape[3]
    degree_count = coef_ref.shape[2]
    degree = lax.broadcasted_iota(jnp.int32, (1, degree_count), 1)
    for w in range(block):
        wave = ids_ref[step * block + w]
        coef = coef_ref[w]
        kept = jnp.where(degree >= wave, coef, jnp.zeros((), coef.dtype))
        prod = lax.dot_general(
            leg_ref[w], kept, (((1,), (1,)), ((), ())), preferred_element_type=jnp.float32
        )
        out_ref[0, :, w, :, :] = prod.astype(out_ref.dtype).reshape(bands, rows, prod.shape[1])


def legendre_transform(local_ids, coef, leg, bands, chunks, chunk):
    local_waves, width, degree_count = coef.shape
    lats = leg.shape[1]
    rows = lats // bands
    chunk_waves = local_waves // chunks
    block = _block_size(chunk_waves)
    steps = chunk_waves // block
    first = chunk * steps
    ids = lax.dynamic_slice_in_dim(local_ids, chunk * chunk_waves, chunk_waves)
    return pl.pallas_call(
        legendre_kernel,
        out_shape=jax.ShapeDtypeStruct((1, bands, chunk_waves, rows, width), jnp.bfloat16),
        grid_spec=pltpu.PrefetchScalarGridSpec(
            num_scalar_prefetch=1,
            grid=(steps,),
            in_specs=[
                pl.BlockSpec((block, width, degree_count), lambda i, ids: (first + i, 0, 0)),
                pl.BlockSpec((block, lats, degree_count), lambda i, ids: (first + i, 0, 0)),
            ],
            out_specs=pl.BlockSpec((1, bands, block, rows, width), lambda i, ids: (0, 0, i, 0, 0)),
        ),
    )(ids, coef, leg)[0]


def per_device(spec_coef, legendre, wave_ids, dep_drow, dep_dlon, dep_frac):
    lat_count = lax.axis_size("lat")
    lon_parts = lax.axis_size("lon")
    local_waves = spec_coef.shape[0]
    level_fields = spec_coef.shape[2]
    degree_count = spec_coef.shape[3]
    all_waves = wave_ids.shape[0]
    row_count = dep_drow.shape[0]
    sector_width = dep_drow.shape[1]
    cycle_size = sector_width * lon_parts
    device = lax.axis_index("lat") * lon_parts + lax.axis_index("lon")
    local_ids = lax.dynamic_slice_in_dim(wave_ids, device * local_waves, local_waves)
    coef = spec_coef.reshape(local_waves, 2 * level_fields, degree_count)
    chunks = 2 if local_waves % 2 == 0 else 1
    chunk_waves = local_waves // chunks
    lon_start = lax.axis_index("lon") * sector_width
    by_chunk = wave_ids.reshape(lat_count, lon_parts, chunks, chunk_waves)
    margin = REACH + 1
    total = None
    for c in range(chunks):
        fourier = legendre_transform(local_ids, coef, legendre, lat_count, chunks, c)
        flat = fourier.reshape(lat_count, chunk_waves * row_count, 2 * level_fields)
        moved = lax.all_to_all(flat, "lat", split_axis=0, concat_axis=0, tiled=True)
        moved = moved.reshape(fourier.shape)
        gathered = lax.all_gather(moved, "lon", axis=0, tiled=True)
        gathered = gathered.reshape(lon_parts * lat_count * chunk_waves, row_count, 2, level_fields)
        wave_order = by_chunk[:, :, c, :].transpose(1, 0, 2).reshape(-1)
        table = wave_table(wave_order, lon_start - margin, sector_width + 2 * margin, cycle_size)
        part = jnp.einsum("mprq,rmx->qpx", gathered, table, preferred_element_type=jnp.float32)
        total = part if total is None else total + part
    wide = total.astype(jnp.bfloat16)
    grid = wide[:, :, margin : margin + sector_width]
    padded = padded_2(wide, (("lat", 1),), margin, False)
    padded = lax.optimization_barrier(padded)
    frac_row = dep_frac[0]
    frac_col = dep_frac[1]
    shifts = range(-REACH, REACH + 2)
    col_weights = [shift_weight(dep_dlon, frac_col, shift) for shift in shifts]
    row_weights = [shift_weight(dep_drow, frac_row, shift) for shift in shifts]
    weights = jnp.stack([r * c for r in row_weights for c in col_weights])
    total = jnp.zeros((level_fields, row_count, sector_width), jnp.float32)
    place = 0
    for row_shift in shifts:
        band = padded[:, margin + row_shift : margin + row_shift + row_count, :]
        for col_shift in shifts:
            window = band[:, :, margin + col_shift : margin + col_shift + sector_width]
            total = total + weights[place][None] * window.astype(jnp.float32)
            place += 1
    return (grid, total.astype(jnp.bfloat16))


def solution(mesh):
    in_specs = (
        P(("lat", "lon"), None, None, None),
        P(("lat", "lon"), None, None),
        P(),
        P("lat", "lon"),
        P("lat", "lon"),
        P(None, "lat", "lon"),
    )
    out_specs = (P(None, "lat", "lon"), P(None, "lat", "lon"))
    return jax.shard_map(
        per_device, mesh=mesh, in_specs=in_specs, out_specs=out_specs, check_vma=False
    )
```

```python
import math

import jax
import jax.numpy as jnp
from jax import lax
from jax.experimental import pallas as pl
from jax.experimental.pallas import tpu as pltpu
from jax.sharding import PartitionSpec as P

REACH = 1


def padded_2(cells, sides, width, closed):
    for axis, dim in sides:
        count = lax.axis_size(axis)
        ends = count if closed else count - 1
        head = lax.slice_in_dim(cells, 0, width, axis=dim)
        tail = lax.slice_in_dim(cells, cells.shape[dim] - width, cells.shape[dim], axis=dim)
        cells = jnp.concatenate(
            [
                lax.ppermute(tail, axis, [(i, (i + 1) % count) for i in range(ends)]),
                cells,
                lax.ppermute(head, axis, [((i + 1) % count, i) for i in range(ends)]),
            ],
            axis=dim,
        )
    return cells


def wave_table(wave_order, lon_start, lon_count, cycle_size):
    inner = 128
    outer = -(-lon_count // inner)
    coarse = lon_start + inner * jnp.arange(outer, dtype=jnp.int32)
    fine = jnp.arange(inner, dtype=jnp.int32)
    scale = 2.0 * math.pi / cycle_size
    theta_a = (wave_order[:, None] * coarse[None, :] % cycle_size).astype(jnp.float32) * scale
    theta_b = (wave_order[:, None] * fine[None, :] % cycle_size).astype(jnp.float32) * scale
    cos_a = jnp.cos(theta_a)[:, :, None]
    sin_a = jnp.sin(theta_a)[:, :, None]
    cos_b = jnp.cos(theta_b)[:, None, :]
    sin_b = jnp.sin(theta_b)[:, None, :]
    factor = jnp.where(wave_order == 0, 1.0, 2.0).astype(jnp.float32)[:, None, None]
    real = factor * (cos_a * cos_b - sin_a * sin_b)
    imag = -factor * (sin_a * cos_b + cos_a * sin_b)
    count = wave_order.shape[0]
    width = outer * inner
    return jnp.stack(
        [real.reshape(count, width)[:, :lon_count], imag.reshape(count, width)[:, :lon_count]]
    ).astype(jnp.bfloat16)


def shift_weight(offsets, frac, shift):
    zeros = jnp.zeros_like(frac)
    lower = jnp.where(offsets == shift, 1.0 - frac, zeros)
    higher = jnp.where(offsets == shift - 1, frac, zeros)
    return lower + higher


def _block_size(count):
    for size in (4, 2, 1):
        if count % size == 0:
            return size
    return 1


def legendre_kernel(ids_ref, coef_ref, leg_ref, out_ref):
    step = pl.program_id(0)
    block = coef_ref.shape[0]
    bands = out_ref.shape[1]
    rows = out_ref.shape[3]
    degree_count = coef_ref.shape[2]
    degree = lax.broadcasted_iota(jnp.int32, (1, degree_count), 1)
    for w in range(block):
        wave = ids_ref[step * block + w]
        coef = coef_ref[w]
        kept = jnp.where(degree >= wave, coef, jnp.zeros((), coef.dtype))
        prod = lax.dot_general(
            leg_ref[w], kept, (((1,), (1,)), ((), ())), preferred_element_type=jnp.float32
        )
        out_ref[0, :, w, :, :] = prod.astype(out_ref.dtype).reshape(bands, rows, prod.shape[1])


def legendre_transform(local_ids, coef, leg, bands, chunks, chunk):
    local_waves, width, degree_count = coef.shape
    lats = leg.shape[1]
    rows = lats // bands
    chunk_waves = local_waves // chunks
    block = _block_size(chunk_waves)
    steps = chunk_waves // block
    first = chunk * steps
    ids = lax.dynamic_slice_in_dim(local_ids, chunk * chunk_waves, chunk_waves)
    return pl.pallas_call(
        legendre_kernel,
        out_shape=jax.ShapeDtypeStruct((1, bands, chunk_waves, rows, width), jnp.bfloat16),
        grid_spec=pltpu.PrefetchScalarGridSpec(
            num_scalar_prefetch=1,
            grid=(steps,),
            in_specs=[
                pl.BlockSpec((block, width, degree_count), lambda i, ids: (first + i, 0, 0)),
                pl.BlockSpec((block, lats, degree_count), lambda i, ids: (first + i, 0, 0)),
            ],
            out_specs=pl.BlockSpec((1, bands, block, rows, width), lambda i, ids: (0, 0, i, 0, 0)),
        ),
    )(ids, coef, leg)[0]


def per_device(spec_coef, legendre, wave_ids, dep_drow, dep_dlon, dep_frac):
    lat_count = lax.axis_size("lat")
    lon_parts = lax.axis_size("lon")
    local_waves = spec_coef.shape[0]
    level_fields = spec_coef.shape[2]
    degree_count = spec_coef.shape[3]
    all_waves = wave_ids.shape[0]
    row_count = dep_drow.shape[0]
    sector_width = dep_drow.shape[1]
    cycle_size = sector_width * lon_parts
    device = lax.axis_index("lat") * lon_parts + lax.axis_index("lon")
    local_ids = lax.dynamic_slice_in_dim(wave_ids, device * local_waves, local_waves)
    coef = spec_coef.reshape(local_waves, 2 * level_fields, degree_count)
    chunks = 2 if local_waves % 2 == 0 else 1
    chunk_waves = local_waves // chunks
    lon_start = lax.axis_index("lon") * sector_width
    by_chunk = wave_ids.reshape(lat_count, lon_parts, chunks, chunk_waves)
    margin = REACH + 1
    total = None
    for c in range(chunks):
        fourier = legendre_transform(local_ids, coef, legendre, lat_count, chunks, c)
        flat = fourier.reshape(lat_count, chunk_waves * row_count, 2 * level_fields)
        moved = lax.all_to_all(flat, "lat", split_axis=0, concat_axis=0, tiled=True)
        moved = moved.reshape(fourier.shape)
        gathered = lax.all_gather(moved, "lon", axis=0, tiled=True)
        gathered = gathered.reshape(lon_parts * lat_count * chunk_waves, row_count, 2, level_fields)
        wave_order = by_chunk[:, :, c, :].transpose(1, 0, 2).reshape(-1)
        table = wave_table(wave_order, lon_start - margin, sector_width + 2 * margin, cycle_size)
        part = jnp.einsum("mprq,rmx->qpx", gathered, table, preferred_element_type=jnp.float32)
        total = part if total is None else total + part
    wide = total.astype(jnp.bfloat16)
    grid = wide[:, :, margin : margin + sector_width]
    padded = padded_2(wide, (("lat", 1),), margin, False)
    padded = lax.optimization_barrier(padded)
    frac_row = dep_frac[0]
    frac_col = dep_frac[1]
    shifts = range(-REACH, REACH + 2)
    col_weights = [shift_weight(dep_dlon, frac_col, shift) for shift in shifts]
    row_weights = [shift_weight(dep_drow, frac_row, shift) for shift in shifts]
    weights = jnp.stack([r * c for r in row_weights for c in col_weights])
    total = jnp.zeros((level_fields, row_count, sector_width), jnp.float32)
    place = 0
    for row_shift in shifts:
        band = padded[:, margin + row_shift : margin + row_shift + row_count, :]
        for col_shift in shifts:
            window = band[:, :, margin + col_shift : margin + col_shift + sector_width]
            total = total + weights[place][None] * window.astype(jnp.float32)
            place += 1
    return (grid, total.astype(jnp.bfloat16))


def solution(mesh):
    in_specs = (
        P(("lat", "lon"), None, None, None),
        P(("lat", "lon"), None, None),
        P(),
        P("lat", "lon"),
        P("lat", "lon"),
        P(None, "lat", "lon"),
    )
    out_specs = (P(None, "lat", "lon"), P(None, "lat", "lon"))
    return jax.shard_map(
        per_device, mesh=mesh, in_specs=in_specs, out_specs=out_specs, check_vma=False
    )
```

```python
import math

import jax
import jax.numpy as jnp
from jax import lax
from jax.experimental import pallas as pl
from jax.experimental.pallas import tpu as pltpu
from jax.sharding import PartitionSpec as P

REACH = 1


def padded_2(cells, sides, width, closed):
    for axis, dim in sides:
        count = lax.axis_size(axis)
        ends = count if closed else count - 1
        head = lax.slice_in_dim(cells, 0, width, axis=dim)
        tail = lax.slice_in_dim(cells, cells.shape[dim] - width, cells.shape[dim], axis=dim)
        cells = jnp.concatenate(
            [
                lax.ppermute(tail, axis, [(i, (i + 1) % count) for i in range(ends)]),
                cells,
                lax.ppermute(head, axis, [((i + 1) % count, i) for i in range(ends)]),
            ],
            axis=dim,
        )
    return cells


def wave_table(wave_order, lon_start, lon_count, cycle_size):
    inner = 128
    outer = -(-lon_count // inner)
    coarse = lon_start + inner * jnp.arange(outer, dtype=jnp.int32)
    fine = jnp.arange(inner, dtype=jnp.int32)
    scale = 2.0 * math.pi / cycle_size
    theta_a = (wave_order[:, None] * coarse[None, :] % cycle_size).astype(jnp.float32) * scale
    theta_b = (wave_order[:, None] * fine[None, :] % cycle_size).astype(jnp.float32) * scale
    cos_a = jnp.cos(theta_a)[:, :, None]
    sin_a = jnp.sin(theta_a)[:, :, None]
    cos_b = jnp.cos(theta_b)[:, None, :]
    sin_b = jnp.sin(theta_b)[:, None, :]
    factor = jnp.where(wave_order == 0, 1.0, 2.0).astype(jnp.float32)[:, None, None]
    real = factor * (cos_a * cos_b - sin_a * sin_b)
    imag = -factor * (sin_a * cos_b + cos_a * sin_b)
    count = wave_order.shape[0]
    width = outer * inner
    return jnp.stack(
        [real.reshape(count, width)[:, :lon_count], imag.reshape(count, width)[:, :lon_count]]
    ).astype(jnp.bfloat16)


def shift_weight(offsets, frac, shift):
    zeros = jnp.zeros_like(frac)
    lower = jnp.where(offsets == shift, 1.0 - frac, zeros)
    higher = jnp.where(offsets == shift - 1, frac, zeros)
    return lower + higher


def _block_size(count):
    for size in (10, 8, 5, 4, 2, 1):
        if count % size == 0:
            return size
    return 1


def legendre_kernel(base_ref, ids_ref, coef_ref, leg_ref, out_ref):
    step = pl.program_id(0)
    block = coef_ref.shape[0]
    bands = out_ref.shape[1]
    rows = out_ref.shape[3]
    degree_count = coef_ref.shape[2]
    degree = lax.broadcasted_iota(jnp.int32, (1, degree_count), 1)
    for w in range(block):
        wave = ids_ref[base_ref[0] + step * block + w]
        coef = coef_ref[w]
        kept = jnp.where(degree >= wave, coef, jnp.zeros((), coef.dtype))
        prod = lax.dot_general(
            leg_ref[w], kept, (((1,), (1,)), ((), ())), preferred_element_type=jnp.float32
        )
        out_ref[0, :, w, :, :] = prod.astype(out_ref.dtype).reshape(bands, rows, prod.shape[1])


def legendre_transform(wave_ids, offset, coef, leg, bands, chunks, chunk):
    local_waves, width, degree_count = coef.shape
    lats = leg.shape[1]
    rows = lats // bands
    chunk_waves = local_waves // chunks
    block = _block_size(chunk_waves)
    steps = chunk_waves // block
    first = chunk * steps
    base = (offset + chunk * chunk_waves).reshape(1)
    return pl.pallas_call(
        legendre_kernel,
        out_shape=jax.ShapeDtypeStruct((1, bands, chunk_waves, rows, width), jnp.bfloat16),
        grid_spec=pltpu.PrefetchScalarGridSpec(
            num_scalar_prefetch=2,
            grid=(steps,),
            in_specs=[
                pl.BlockSpec((block, width, degree_count), lambda i, base, ids: (first + i, 0, 0)),
                pl.BlockSpec((block, lats, degree_count), lambda i, base, ids: (first + i, 0, 0)),
            ],
            out_specs=pl.BlockSpec((1, bands, block, rows, width), lambda i, base, ids: (0, 0, i, 0, 0)),
        ),
    )(base, wave_ids, coef, leg)[0]


def per_device(spec_coef, legendre, wave_ids, dep_drow, dep_dlon, dep_frac):
    lat_count = lax.axis_size("lat")
    lon_parts = lax.axis_size("lon")
    local_waves = spec_coef.shape[0]
    level_fields = spec_coef.shape[2]
    degree_count = spec_coef.shape[3]
    all_waves = wave_ids.shape[0]
    row_count = dep_drow.shape[0]
    sector_width = dep_drow.shape[1]
    cycle_size = sector_width * lon_parts
    device = lax.axis_index("lat") * lon_parts + lax.axis_index("lon")
    offset = (device * local_waves).astype(jnp.int32)
    coef = spec_coef.reshape(local_waves, 2 * level_fields, degree_count)
    chunks = 2 if local_waves % 2 == 0 else 1
    chunk_waves = local_waves // chunks
    lon_start = lax.axis_index("lon") * sector_width
    by_chunk = wave_ids.reshape(lat_count, lon_parts, chunks, chunk_waves)
    margin = REACH + 1
    total = None
    for c in range(chunks):
        fourier = legendre_transform(wave_ids, offset, coef, legendre, lat_count, chunks, c)
        flat = fourier.reshape(lat_count, chunk_waves * row_count, 2 * level_fields)
        moved = lax.all_to_all(flat, "lat", split_axis=0, concat_axis=0, tiled=True)
        moved = moved.reshape(fourier.shape)
        gathered = lax.all_gather(moved, "lon", axis=0, tiled=True)
        gathered = gathered.reshape(lon_parts * lat_count * chunk_waves, row_count, 2, level_fields)
        wave_order = by_chunk[:, :, c, :].transpose(1, 0, 2).reshape(-1)
        table = wave_table(wave_order, lon_start - margin, sector_width + 2 * margin, cycle_size)
        part = jnp.einsum("mprq,rmx->qpx", gathered, table, preferred_element_type=jnp.float32)
        total = part if total is None else total + part
    wide = total.astype(jnp.bfloat16)
    grid = wide[:, :, margin : margin + sector_width]
    padded = padded_2(wide, (("lat", 1),), margin, False)
    padded = lax.optimization_barrier(padded)
    frac_row = dep_frac[0]
    frac_col = dep_frac[1]
    shifts = range(-REACH, REACH + 2)
    col_weights = [shift_weight(dep_dlon, frac_col, shift) for shift in shifts]
    row_weights = [shift_weight(dep_drow, frac_row, shift) for shift in shifts]
    weights = jnp.stack([r * c for r in row_weights for c in col_weights])
    total = jnp.zeros((level_fields, row_count, sector_width), jnp.float32)
    place = 0
    for row_shift in shifts:
        band = padded[:, margin + row_shift : margin + row_shift + row_count, :]
        for col_shift in shifts:
            window = band[:, :, margin + col_shift : margin + col_shift + sector_width]
            total = total + weights[place][None] * window.astype(jnp.float32)
            place += 1
    return (grid, total.astype(jnp.bfloat16))


def solution(mesh):
    in_specs = (
        P(("lat", "lon"), None, None, None),
        P(("lat", "lon"), None, None),
        P(),
        P("lat", "lon"),
        P("lat", "lon"),
        P(None, "lat", "lon"),
    )
    out_specs = (P(None, "lat", "lon"), P(None, "lat", "lon"))
    return jax.shard_map(
        per_device, mesh=mesh, in_specs=in_specs, out_specs=out_specs, check_vma=False
    )
```
